256 devices in a mesh: cfg: 2 (over x_hi), seq: 32 (over x_lo, z, core), tp: 4 (over y).
Axes of the slice: x: 4 (x_hi: 2, x_lo: 2; x = x_hi * 2 + x_lo), y: 4, z: 8, core: 2. Of those that a mesh axis runs over, the one named last changes fastest.
Arguments:
- img_hidden: bfloat16 [2, 1024, 8, 1536], P('cfg', 'seq'), may hold values from -80 to 80
- txt_hidden: bfloat16 [2, 160, 8, 1536], P('cfg', 'seq'), may hold values from -6 to 6
- modulation: bfloat16 [2, 8, 10, 1536], P('cfg'), may hold values from -3 to 5
- text_lengths: int32 [2, 8], P('cfg'), may hold values from 1 to 160, as said below
- timestep_index: int32 [8], replicated, may hold values from 0 to 7
- sigmas: float32 [9], replicated, may hold values from 0 to 2, as said below
- latents: float32 [1024, 8, 64], P(('seq', 'tp'), None, 'cfg'), may hold values from -6 to 6
- w_qkv: bfloat16 [1536, 3, 1536], P(None, None, 'tp'), may hold values from -0.3125 to 0.3125
- w_kv_text: bfloat16 [1536, 2, 1536], P(None, None, 'tp'), may hold values from -0.3125 to 0.3125
- w_out: bfloat16 [1536, 1536], P('tp'), may hold values from -0.15625 to 0.15625
- w_up: bfloat16 [1536, 3072], P(None, 'tp'), may hold values from -0.15625 to 0.15625
- w_down: bfloat16 [3072, 1536], P('tp'), may hold values from -0.109375 to 0.109375
- w_final: bfloat16 [1536, 64], replicated, may hold values from -0.15625 to 0.15625
Outputs:
- velocity: float32 [1024, 8, 64], P(('seq', 'tp'), None, 'cfg')
- latent_next: float32 [1024, 8, 64], P(('seq', 'tp'), None, 'cfg')
The draws below stay inside these ranges and needn't reach their ends.
Inputs may be any that keep to these rules, and one draw needn't show every extreme that they name: `text_lengths`: in every draw the conditional copy of some request fills all 160 text slots. `sigmas`: Falling; each step down lies between 0.5 / 8 and 1.5 / 8.
All inputs are finite; a program needn't handle non-finite values.
Results may differ from the reference program's by a relative error of at most 0.014.
The reference program's roundings to bfloat16 on the way count: a program that leaves them out, or rounds other values in their place, can miss the bound.
Values may be sent and summed in bfloat16 or wider, within the bound.
No kernel may reach another device: no remote copies, remote signals or barrier semaphores. Data moves between devices by JAX's collectives and lax.ppermute only.
A program may use at most 128 MiB of HBM per device.

```python
import math
import jax
import jax.numpy as jnp
from jax import lax

D = 1536
HEADS = 24
HEAD_DIM = 64
PATCH = 64
FF = 3072
TXT = 160
STEPS = 8
IMG = 1024
REQ = 8
N_TP = 4


def draw_img_hidden(key, part):
    key_base, key_rows, key_cols = jax.random.split(key, 3)
    base_values = jnp.clip(jax.random.normal(key_base, (2, IMG, REQ, D), jnp.float32), -4.0, 4.0)
    row_scale = jnp.exp(jax.random.uniform(key_rows, (2, IMG, REQ, 1), jnp.float32, 0.0, math.log(10.0)))
    column_scale = jnp.exp(jax.random.uniform(key_cols, (1, 1, 1, D), jnp.float32, math.log(0.5), math.log(2.0)))
    return (base_values * row_scale * column_scale).astype(jnp.bfloat16)


def draw_modulation(key, part):
    values_all = jnp.clip(0.5 * jax.random.normal(key, (2, REQ, 10, D), jnp.float32), -3.0, 3.0)
    return values_all.astype(jnp.bfloat16)


def draw_text_lengths(key, part):
    key_lengths, key_choice = jax.random.split(key)
    lengths_all = jax.random.randint(key_lengths, (2, REQ), 1, TXT + 1)
    chosen = jax.random.randint(key_choice, (), 0, REQ)
    full_slot = (jnp.arange(2)[:, None] == 0) & (jnp.arange(REQ)[None, :] == chosen)
    return jnp.where(full_slot, TXT, lengths_all).astype(jnp.int32)


def draw_sigmas(key, part):
    jitter = jax.random.uniform(key, (STEPS + 1,), jnp.float32)
    position = jnp.arange(STEPS + 1).astype(jnp.float32)
    return (STEPS - position + 0.5 * jitter) / STEPS


def with_ends(result, own_key, smallest, largest):
    extent = result.shape
    place = [jax.random.randint(jax.random.fold_in(own_key, axis), (), 0, extent[axis]) for axis in range(len(extent))]
    result = result.at[tuple(place)].set(smallest)
    longest = extent.index(max(extent))
    place[longest] = (place[longest] + 1) % extent[longest]
    return result.at[tuple(place)].set(largest)


def levels(key, dims, pieces, least, largest):
    gain, own = 1.0, jax.random.fold_in(key, 6)
    for dim, shards_of in pieces:
        steps = jnp.exp(jax.random.uniform(jax.random.fold_in(own, dim), (shards_of,), jnp.float32, least / len(pieces), largest / len(pieces)))
        gain = gain * jnp.repeat(steps, dims[dim] // shards_of).reshape([-1 if axis == dim else 1 for axis in range(len(dims))])
    return gain


def normal_values(stream_key, shape, deviation, bound, cuts=(), kind=jnp.bfloat16):
    array = jax.random.normal(stream_key, shape, jnp.float32) * deviation
    if len(cuts) > 0:
        array = levels(stream_key, shape, cuts, -0.22, 0.18) * array
    return jnp.clip(array, min=-bound, max=bound).astype(kind)


def setup_inputs(seed: int = 0) -> dict:
    arg_keys = jax.random.split(jax.random.key(seed), 14)
    img_hidden = draw_img_hidden(jax.random.fold_in(arg_keys[13], 71), 0)
    txt_hidden = normal_values(arg_keys[1], (2, TXT, REQ, D), 1.0, 6.0, ((0, 2), (1, 32)))
    modulation = draw_modulation(jax.random.fold_in(arg_keys[13], 71), 0)
    text_lengths = draw_text_lengths(jax.random.fold_in(arg_keys[13], 71), 0)
    timestep_index = with_ends(jax.random.randint(arg_keys[4], (REQ,), 0, STEPS), jax.random.fold_in(arg_keys[4], 1), 0, STEPS - 1).astype(jnp.int32)
    sigmas = draw_sigmas(jax.random.fold_in(arg_keys[13], 71), 0)
    latents = normal_values(arg_keys[6], (IMG, REQ, PATCH), 1.0, 6.0, ((0, 128), (2, 2)), jnp.float32)
    w_qkv = normal_values(arg_keys[7], (D, 3, D), (D // 4) ** -0.5, 0.3125, ((2, 4),))
    w_kv_text = normal_values(arg_keys[8], (D, 2, D), (D // 4) ** -0.5, 0.3125, ((2, 4),))
    w_out = normal_values(arg_keys[9], (D, D), D ** -0.5, 0.15625, ((0, 4),))
    w_up = normal_values(arg_keys[10], (D, FF), D ** -0.5, 0.15625, ((1, 4),))
    w_down = normal_values(arg_keys[11], (FF, D), FF ** -0.5, 0.109375, ((0, 4),))
    w_final = normal_values(arg_keys[12], (D, PATCH), D ** -0.5, 0.15625)
    return dict(img_hidden=img_hidden, txt_hidden=txt_hidden, modulation=modulation, text_lengths=text_lengths, timestep_index=timestep_index, sigmas=sigmas, latents=latents, w_qkv=w_qkv, w_kv_text=w_kv_text, w_out=w_out, w_up=w_up, w_down=w_down, w_final=w_final)


EPSILON = 1e-06
GUIDANCE = 7.0

def layer_norm(values):
    center = values - lax.optimization_barrier(jnp.mean(values, -1, keepdims=True))
    return center * lax.rsqrt(lax.optimization_barrier(jnp.mean(center * center, -1, keepdims=True)) + EPSILON)

def modulate(values, shift_add, scale_mul):
    return (layer_norm(values) * (1.0 + scale_mul) + shift_add).astype(jnp.bfloat16)

def softmax_rows(scores):
    row_max = lax.optimization_barrier(jnp.max(scores, -1, keepdims=True))
    exp_scores = jnp.exp(scores - row_max)
    return exp_scores / lax.optimization_barrier(jnp.sum(exp_scores, -1, keepdims=True))

def grouped_product(left_side, right_side):
    part_size = left_side.shape[1] // N_TP
    running_sum = jnp.zeros((left_side.shape[0], right_side.shape[1]), jnp.float32)
    for member in range(N_TP):
        partial_term = jnp.dot(left_side[:, member * part_size:(member + 1) * part_size], right_side[member * part_size:(member + 1) * part_size], preferred_element_type=jnp.float32)
        running_sum = running_sum + lax.optimization_barrier(partial_term.astype(jnp.bfloat16)).astype(jnp.float32)
    return running_sum

def reference(img_hidden, txt_hidden, modulation, text_lengths, timestep_index, sigmas, latents, w_qkv, w_kv_text, w_out, w_up, w_down, w_final):
    qkv_matrix = w_qkv.reshape(D, 3 * D)
    text_matrix = w_kv_text.reshape(D, 2 * D)
    scaling = 1.0 / math.sqrt(HEAD_DIM)

    def one_request(flat_index):
        cfg_copy = (flat_index // REQ).astype(jnp.int32)
        request = (flat_index % REQ).astype(jnp.int32)
        image_rows = lax.dynamic_index_in_dim(lax.dynamic_index_in_dim(img_hidden, cfg_copy, 0, False), request, 1, False).astype(jnp.float32)
        text_rows = lax.dynamic_index_in_dim(lax.dynamic_index_in_dim(txt_hidden, cfg_copy, 0, False), request, 1, False).astype(jnp.float32)
        adaptive = lax.dynamic_index_in_dim(lax.dynamic_index_in_dim(modulation, cfg_copy, 0, False), request, 0, False).astype(jnp.float32)
        length_now = lax.dynamic_index_in_dim(lax.dynamic_index_in_dim(text_lengths, cfg_copy, 0, False), request, 0, False)
        normed = modulate(image_rows, adaptive[0], adaptive[1])
        projected = jnp.dot(normed, qkv_matrix, preferred_element_type=jnp.float32).astype(jnp.bfloat16)
        projected = lax.optimization_barrier(projected)
        text_kv = jnp.dot(modulate(text_rows, adaptive[6], adaptive[7]), text_matrix, preferred_element_type=jnp.float32).astype(jnp.bfloat16)
        text_kv = lax.optimization_barrier(text_kv)
        queries = projected[:, :D].reshape(IMG, HEADS, HEAD_DIM).astype(jnp.float32)
        keys_all = jnp.concatenate([projected[:, D:2 * D], text_kv[:, :D]], 0).reshape(IMG + TXT, HEADS, HEAD_DIM).astype(jnp.float32)
        values_all = jnp.concatenate([projected[:, 2 * D:], text_kv[:, D:]], 0).reshape(IMG + TXT, HEADS, HEAD_DIM).astype(jnp.float32)
        key_valid = jnp.concatenate([jnp.ones((IMG,), bool), jnp.arange(TXT, dtype=jnp.int32) < length_now])
        scores = jnp.einsum('qhd,khd->hqk', queries, keys_all) * scaling
        scores = jnp.where(key_valid[None, None, :], scores, -jnp.inf)
        weights = lax.optimization_barrier(softmax_rows(scores).astype(jnp.bfloat16)).astype(jnp.float32)
        attention = jnp.einsum('hqk,khd->qhd', weights, values_all).astype(jnp.bfloat16).reshape(IMG, D)
        after_attn = image_rows + adaptive[2] * grouped_product(attention, w_out)
        mlp_in = modulate(after_attn, adaptive[3], adaptive[4])
        hidden = jax.nn.gelu(jnp.dot(mlp_in, w_up, preferred_element_type=jnp.float32), approximate=True).astype(jnp.bfloat16)
        after_mlp = after_attn + adaptive[5] * grouped_product(hidden, w_down)
        head_in = modulate(after_mlp, adaptive[8], adaptive[9])
        return jnp.dot(head_in, w_final, preferred_element_type=jnp.float32)
    outputs = lax.map(one_request, jnp.arange(2 * REQ, dtype=jnp.int32))
    per_copy = outputs.reshape(2, REQ, IMG, PATCH).transpose(0, 2, 1, 3)
    velocity = per_copy[1] + GUIDANCE * (per_copy[0] - per_copy[1])
    steps_all = jnp.arange(STEPS + 1, dtype=jnp.int32)
    sigma_now = lax.optimization_barrier(jnp.sum(jnp.where(steps_all[None, :] == timestep_index[:, None], sigmas[None, :], 0.0), 1))
    sigma_after = lax.optimization_barrier(jnp.sum(jnp.where(steps_all[None, :] == timestep_index[:, None] + 1, sigmas[None, :], 0.0), 1))
    latent_next = latents + (sigma_after - sigma_now)[None, :, None] * velocity
    return (velocity, latent_next)
```

```python
import math

import jax
import jax.numpy as jnp
from jax import lax
from jax.sharding import PartitionSpec as P

HEAD_DIM = 64


EPSILON = 1e-06
GUIDANCE = 7.0


def swapped(value, axis, apart):
    return lax.ppermute(value, axis, [(i, i ^ 1 << apart) for i in range(lax.axis_size(axis))])


def layer_norm(values):
    center = values - jnp.mean(values, -1, keepdims=True)
    return center * lax.rsqrt(jnp.mean(center * center, -1, keepdims=True) + EPSILON)


def modulate(values, shift_add, scale_mul):
    return (layer_norm(values) * (1.0 + scale_mul) + shift_add).astype(jnp.bfloat16)


def attend(queries, keys_in, values_in, key_valid):
    heads = queries.shape[2] // HEAD_DIM
    query_heads = queries.reshape(queries.shape[0], queries.shape[1], heads, HEAD_DIM)
    key_heads = keys_in.reshape(keys_in.shape[0], keys_in.shape[1], heads, HEAD_DIM)
    value_heads = values_in.reshape(values_in.shape[0], values_in.shape[1], heads, HEAD_DIM)
    scores = jnp.einsum(
        "qrhd,krhd->rhqk", query_heads, key_heads, preferred_element_type=jnp.float32
    ) * (1.0 / math.sqrt(HEAD_DIM))
    scores = jnp.where(key_valid[:, None, None, :], scores, -jnp.inf)
    row_max = jnp.max(scores, -1, keepdims=True)
    exp_scores = jnp.exp(scores - row_max)
    weights = (exp_scores / jnp.sum(exp_scores, -1, keepdims=True)).astype(jnp.bfloat16)
    result = jnp.einsum("rhqk,krhd->qrhd", weights, value_heads, preferred_element_type=jnp.float32)
    return result.astype(jnp.bfloat16).reshape(queries.shape)


def reduce_rows(partial, parties):
    pieces = partial.reshape(parties, partial.shape[0] // parties, partial.shape[1])
    got = lax.all_to_all(pieces, "tp", split_axis=0, concat_axis=0, tiled=True)
    return jnp.sum(got.astype(jnp.float32), 0)


def spread(image_part, text_part, members):
    joined = jnp.concatenate([image_part, text_part], 0).transpose(1, 0, 2)
    widened = jnp.broadcast_to(joined[:, None], (joined.shape[0], members) + joined.shape[1:])
    return widened.reshape(joined.shape[0] * members, joined.shape[1], joined.shape[2])


def shards(
    img_hidden,
    txt_hidden,
    modulation,
    text_lengths,
    timestep_index,
    sigmas,
    latents,
    w_qkv,
    w_kv_text,
    w_out,
    w_up,
    w_down,
    w_final,
):
    img_slice = img_hidden.shape[1]
    requests = img_hidden.shape[2]
    model_width = img_hidden.shape[3]
    txt_slice = txt_hidden.shape[1]
    features = w_out.shape[0]
    members = lax.axis_size("seq") // requests
    parties = lax.axis_size("tp")
    portion = img_slice // parties
    rows_all = img_slice * requests
    adaptive = modulation[0].astype(jnp.float32)
    resident = img_hidden[0].astype(jnp.float32)
    lengths_all = text_lengths[0]
    normed = modulate(resident, adaptive[:, 0], adaptive[:, 1]).reshape(rows_all, model_width)
    projected = jnp.dot(
        normed, w_qkv.reshape(model_width, 3 * features), preferred_element_type=jnp.float32
    ).astype(jnp.bfloat16)
    queries = projected[:, :features].reshape(img_slice, requests, features)
    keys_img = projected[:, features : 2 * features].reshape(img_slice, requests, features)
    vals_img = projected[:, 2 * features :].reshape(img_slice, requests, features)
    text_in = modulate(txt_hidden[0].astype(jnp.float32), adaptive[:, 6], adaptive[:, 7]).reshape(
        txt_slice * requests, model_width
    )
    text_kv = jnp.dot(
        text_in, w_kv_text.reshape(model_width, 2 * features), preferred_element_type=jnp.float32
    ).astype(jnp.bfloat16)
    keys_txt = text_kv[:, :features].reshape(txt_slice, requests, features)
    vals_txt = text_kv[:, features:].reshape(txt_slice, requests, features)
    key_span = img_slice + txt_slice
    within = jnp.arange(key_span)
    query_share = img_slice // members
    senders = requests * members
    query_send = (
        queries.reshape(members, query_share, requests, features)
        .transpose(2, 0, 1, 3)
        .reshape(senders, query_share, features)
    )
    key_send = spread(keys_img, keys_txt, members)
    value_send = spread(vals_img, vals_txt, members)
    query_got, key_got, value_got = (
        lax.all_to_all(query_send, "seq", split_axis=0, concat_axis=0, tiled=True),
        lax.all_to_all(key_send, "seq", split_axis=0, concat_axis=0, tiled=True),
        lax.all_to_all(value_send, "seq", split_axis=0, concat_axis=0, tiled=True),
    )
    my_request = lax.axis_index("seq") // members
    length_now = jnp.sum(jnp.where(jnp.arange(requests) == my_request, lengths_all, 0))
    text_slot = jnp.arange(senders)[:, None] * txt_slice + within[None, :] - img_slice
    key_valid = (within[None, :] < img_slice) | (text_slot < length_now)
    answer = attend(
        query_got.reshape(senders * query_share, 1, features),
        key_got.reshape(senders * key_span, 1, features),
        value_got.reshape(senders * key_span, 1, features),
        key_valid.reshape(1, senders * key_span),
    )
    answer_back = lax.all_to_all(
        answer.reshape(senders, query_share, features),
        "seq",
        split_axis=0,
        concat_axis=0,
        tiled=True,
    )
    attn_rows = (
        answer_back.reshape(requests, members, query_share, features)
        .transpose(1, 2, 0, 3)
        .reshape(rows_all, features)
    )
    tp_index = lax.axis_index("tp")
    resident_mine = lax.dynamic_slice_in_dim(resident, tp_index * portion, portion, 0)
    attn_part = jnp.dot(attn_rows, w_out, preferred_element_type=jnp.float32).astype(jnp.bfloat16)
    attn_mixed = reduce_rows(attn_part, parties).reshape(portion, requests, model_width)
    after_attn = resident_mine + adaptive[:, 2] * attn_mixed
    mlp_mine = modulate(after_attn, adaptive[:, 3], adaptive[:, 4])
    mlp_in = lax.all_gather(mlp_mine, "tp", axis=0, tiled=True).reshape(rows_all, model_width)
    hidden = jax.nn.gelu(
        jnp.dot(mlp_in, w_up, preferred_element_type=jnp.float32), approximate=True
    ).astype(jnp.bfloat16)
    mlp_part = jnp.dot(hidden, w_down, preferred_element_type=jnp.float32).astype(jnp.bfloat16)
    mlp_grown = reduce_rows(mlp_part, parties).reshape(portion, requests, model_width)
    after_mlp = after_attn + adaptive[:, 5] * mlp_grown
    head_in = modulate(after_mlp, adaptive[:, 8], adaptive[:, 9]).reshape(
        portion * requests, model_width
    )
    velocity_own = jnp.dot(head_in, w_final, preferred_element_type=jnp.float32).reshape(
        portion, requests, w_final.shape[1]
    )
    half_width = w_final.shape[1] // 2
    cfg_index = lax.axis_index("cfg")
    own_kept = lax.dynamic_slice_in_dim(velocity_own, cfg_index * half_width, half_width, 2)
    own_given = lax.dynamic_slice_in_dim(velocity_own, (1 - cfg_index) * half_width, half_width, 2)
    velocity_other = swapped(own_given, "cfg", 0)
    is_first = cfg_index == 0
    guided_cond = jnp.where(is_first, own_kept, velocity_other)
    guided_free = jnp.where(is_first, velocity_other, own_kept)
    velocity = guided_free + GUIDANCE * (guided_cond - guided_free)
    steps_all = jnp.arange(sigmas.shape[0], dtype=jnp.int32)
    sigma_now = jnp.sum(
        jnp.where(steps_all[None, :] == timestep_index[:, None], sigmas[None, :], 0.0), 1
    )
    sigma_after = jnp.sum(
        jnp.where(steps_all[None, :] == timestep_index[:, None] + 1, sigmas[None, :], 0.0), 1
    )
    latent_next = latents + (sigma_after - sigma_now)[None, :, None] * velocity
    return (velocity, latent_next)


def solution(mesh):
    return jax.shard_map(
        shards,
        mesh=mesh,
        in_specs=(
            P("cfg", "seq", None, None),
            P("cfg", "seq", None, None),
            P("cfg", None, None, None),
            P("cfg", None),
            P(),
            P(),
            P(("seq", "tp"), None, "cfg"),
            P(None, None, "tp"),
            P(None, None, "tp"),
            P("tp", None),
            P(None, "tp"),
            P("tp", None),
            P(),
        ),
        out_specs=(P(("seq", "tp"), None, "cfg"), P(("seq", "tp"), None, "cfg")),
        check_vma=False,
    )
```

```python
import math

import jax
import jax.numpy as jnp
from jax import lax
from jax.sharding import PartitionSpec as P

HEAD_DIM = 64


EPSILON = 1e-06
GUIDANCE = 7.0


def swapped(value, axis, apart):
    return lax.ppermute(value, axis, [(i, i ^ 1 << apart) for i in range(lax.axis_size(axis))])


def layer_norm(values):
    center = values - jnp.mean(values, -1, keepdims=True)
    return center * lax.rsqrt(jnp.mean(center * center, -1, keepdims=True) + EPSILON)


def modulate(values, shift_add, scale_mul):
    return (layer_norm(values) * (1.0 + scale_mul) + shift_add).astype(jnp.bfloat16)


def attend(queries, keys_in, values_in, key_valid):
    heads = queries.shape[2] // HEAD_DIM
    query_heads = queries.reshape(queries.shape[0], queries.shape[1], heads, HEAD_DIM)
    key_heads = keys_in.reshape(keys_in.shape[0], keys_in.shape[1], heads, HEAD_DIM)
    value_heads = values_in.reshape(values_in.shape[0], values_in.shape[1], heads, HEAD_DIM)
    scores = jnp.einsum(
        "qrhd,krhd->rhqk", query_heads, key_heads, preferred_element_type=jnp.float32
    ) * (1.0 / math.sqrt(HEAD_DIM))
    scores = jnp.where(key_valid[:, None, None, :], scores, -jnp.inf)
    row_max = jnp.max(scores, -1, keepdims=True)
    exp_scores = jnp.exp(scores - row_max)
    weights = (exp_scores / jnp.sum(exp_scores, -1, keepdims=True)).astype(jnp.bfloat16)
    result = jnp.einsum("rhqk,krhd->qrhd", weights, value_heads, preferred_element_type=jnp.float32)
    return result.astype(jnp.bfloat16).reshape(queries.shape)


def reduce_rows(partial, parties):
    pieces = partial.reshape(parties, partial.shape[0] // parties, partial.shape[1])
    got = lax.all_to_all(pieces, "tp", split_axis=0, concat_axis=0, tiled=True)
    return jnp.sum(got.astype(jnp.float32), 0)


def spread(image_part, text_part, members):
    joined = jnp.concatenate([image_part, text_part], 0).transpose(1, 0, 2)
    widened = jnp.broadcast_to(joined[:, None], (joined.shape[0], members) + joined.shape[1:])
    return widened.reshape(joined.shape[0] * members, joined.shape[1], joined.shape[2])


def shards(
    img_hidden,
    txt_hidden,
    modulation,
    text_lengths,
    timestep_index,
    sigmas,
    latents,
    w_qkv,
    w_kv_text,
    w_out,
    w_up,
    w_down,
    w_final,
):
    img_slice = img_hidden.shape[1]
    requests = img_hidden.shape[2]
    model_width = img_hidden.shape[3]
    txt_slice = txt_hidden.shape[1]
    features = w_out.shape[0]
    members = lax.axis_size("seq") // requests
    parties = lax.axis_size("tp")
    portion = img_slice // parties
    rows_all = img_slice * requests
    adaptive = modulation[0].astype(jnp.float32)
    resident = img_hidden[0].astype(jnp.float32)
    lengths_all = text_lengths[0]
    normed = modulate(resident, adaptive[:, 0], adaptive[:, 1]).reshape(rows_all, model_width)
    projected = jnp.dot(
        normed, w_qkv.reshape(model_width, 3 * features), preferred_element_type=jnp.float32
    ).astype(jnp.bfloat16)
    queries = projected[:, :features].reshape(img_slice, requests, features)
    keys_img = projected[:, features : 2 * features].reshape(img_slice, requests, features)
    vals_img = projected[:, 2 * features :].reshape(img_slice, requests, features)
    text_in = modulate(txt_hidden[0].astype(jnp.float32), adaptive[:, 6], adaptive[:, 7]).reshape(
        txt_slice * requests, model_width
    )
    text_kv = jnp.dot(
        text_in, w_kv_text.reshape(model_width, 2 * features), preferred_element_type=jnp.float32
    ).astype(jnp.bfloat16)
    keys_txt = text_kv[:, :features].reshape(txt_slice, requests, features)
    vals_txt = text_kv[:, features:].reshape(txt_slice, requests, features)
    key_span = img_slice + txt_slice
    within = jnp.arange(key_span)
    senders = requests * members
    halves = members // 2
    query_share = img_slice // halves
    head_share = features // 2
    query_send = (
        queries.reshape(halves, query_share, requests, 2, head_share)
        .transpose(2, 0, 3, 1, 4)
        .reshape(senders, query_share, head_share)
    )
    joined_k = jnp.concatenate([keys_img, keys_txt], 0).reshape(key_span, requests, 2, head_share)
    joined_v = jnp.concatenate([vals_img, vals_txt], 0).reshape(key_span, requests, 2, head_share)
    both = jnp.concatenate([joined_k, joined_v], 0).transpose(1, 2, 0, 3)
    kv_send = jnp.broadcast_to(
        both[:, None], (requests, halves, 2, 2 * key_span, head_share)
    ).reshape(senders, 2 * key_span, head_share)
    payload = jnp.concatenate([query_send, kv_send], 1)
    got = lax.all_to_all(payload, "seq", split_axis=0, concat_axis=0, tiled=True)
    query_got = got[:, :query_share]
    key_got = got[:, query_share : query_share + key_span]
    value_got = got[:, query_share + key_span :]
    my_request = lax.axis_index("seq") // members
    length_now = jnp.sum(jnp.where(jnp.arange(requests) == my_request, lengths_all, 0))
    text_slot = jnp.arange(senders)[:, None] * txt_slice + within[None, :] - img_slice
    key_valid = (within[None, :] < img_slice) | (text_slot < length_now)
    answer = attend(
        query_got.reshape(senders * query_share, 1, head_share),
        key_got.reshape(senders * key_span, 1, head_share),
        value_got.reshape(senders * key_span, 1, head_share),
        key_valid.reshape(1, senders * key_span),
    )
    answer_back = lax.all_to_all(
        answer.reshape(senders, query_share, head_share),
        "seq",
        split_axis=0,
        concat_axis=0,
        tiled=True,
    )
    attn_rows = (
        answer_back.reshape(requests, halves, 2, query_share, head_share)
        .transpose(1, 3, 0, 2, 4)
        .reshape(rows_all, features)
    )
    tp_index = lax.axis_index("tp")
    resident_mine = lax.dynamic_slice_in_dim(resident, tp_index * portion, portion, 0)
    attn_part = jnp.dot(attn_rows, w_out, preferred_element_type=jnp.float32).astype(jnp.bfloat16)
    attn_mixed = reduce_rows(attn_part, parties).reshape(portion, requests, model_width)
    after_attn = resident_mine + adaptive[:, 2] * attn_mixed
    mlp_mine = modulate(after_attn, adaptive[:, 3], adaptive[:, 4])
    mlp_in = lax.all_gather(mlp_mine, "tp", axis=0, tiled=True).reshape(rows_all, model_width)
    hidden = jax.nn.gelu(
        jnp.dot(mlp_in, w_up, preferred_element_type=jnp.float32), approximate=True
    ).astype(jnp.bfloat16)
    mlp_part = jnp.dot(hidden, w_down, preferred_element_type=jnp.float32).astype(jnp.bfloat16)
    mlp_grown = reduce_rows(mlp_part, parties).reshape(portion, requests, model_width)
    after_mlp = after_attn + adaptive[:, 5] * mlp_grown
    head_in = modulate(after_mlp, adaptive[:, 8], adaptive[:, 9]).reshape(
        portion * requests, model_width
    )
    velocity_own = jnp.dot(head_in, w_final, preferred_element_type=jnp.float32).reshape(
        portion, requests, w_final.shape[1]
    )
    half_width = w_final.shape[1] // 2
    cfg_index = lax.axis_index("cfg")
    own_kept = lax.dynamic_slice_in_dim(velocity_own, cfg_index * half_width, half_width, 2)
    own_given = lax.dynamic_slice_in_dim(velocity_own, (1 - cfg_index) * half_width, half_width, 2)
    velocity_other = swapped(own_given, "cfg", 0)
    is_first = cfg_index == 0
    guided_cond = jnp.where(is_first, own_kept, velocity_other)
    guided_free = jnp.where(is_first, velocity_other, own_kept)
    velocity = guided_free + GUIDANCE * (guided_cond - guided_free)
    steps_all = jnp.arange(sigmas.shape[0], dtype=jnp.int32)
    sigma_now = jnp.sum(
        jnp.where(steps_all[None, :] == timestep_index[:, None], sigmas[None, :], 0.0), 1
    )
    sigma_after = jnp.sum(
        jnp.where(steps_all[None, :] == timestep_index[:, None] + 1, sigmas[None, :], 0.0), 1
    )
    latent_next = latents + (sigma_after - sigma_now)[None, :, None] * velocity
    return (velocity, latent_next)


def solution(mesh):
    return jax.shard_map(
        shards,
        mesh=mesh,
        in_specs=(
            P("cfg", "seq", None, None),
            P("cfg", "seq", None, None),
            P("cfg", None, None, None),
            P("cfg", None),
            P(),
            P(),
            P(("seq", "tp"), None, "cfg"),
            P(None, None, "tp"),
            P(None, None, "tp"),
            P("tp", None),
            P(None, "tp"),
            P("tp", None),
            P(),
        ),
        out_specs=(P(("seq", "tp"), None, "cfg"), P(("seq", "tp"), None, "cfg")),
        check_vma=False,
    )
```

```python
import math

import jax
import jax.numpy as jnp
from jax import lax
from jax.sharding import PartitionSpec as P

HEAD_DIM = 64


EPSILON = 1e-06
GUIDANCE = 7.0


def swapped(value, axis, apart):
    return lax.ppermute(value, axis, [(i, i ^ 1 << apart) for i in range(lax.axis_size(axis))])


def layer_norm(values):
    center = values - jnp.mean(values, -1, keepdims=True)
    return center * lax.rsqrt(jnp.mean(center * center, -1, keepdims=True) + EPSILON)


def modulate(values, shift_add, scale_mul):
    return (layer_norm(values) * (1.0 + scale_mul) + shift_add).astype(jnp.bfloat16)


def attend(queries, keys_img, values_img, keys_txt, values_txt, text_valid):
    width = queries.shape[1]
    heads = width // HEAD_DIM
    chosen = (jnp.arange(width)[None, :] // HEAD_DIM) == jnp.arange(heads)[:, None]
    query_heads = jnp.where(chosen[:, None, :], queries[None], 0).astype(queries.dtype)
    scale = 1.0 / math.sqrt(HEAD_DIM)
    scores_img = (
        jnp.einsum("hqf,kf->hqk", query_heads, keys_img, preferred_element_type=jnp.float32) * scale
    )
    scores_txt = (
        jnp.einsum("hqf,kf->hqk", query_heads, keys_txt, preferred_element_type=jnp.float32) * scale
    )
    scores_txt = jnp.where(text_valid[None, None, :], scores_txt, -jnp.inf)
    row_max = jnp.maximum(
        jnp.max(scores_img, -1, keepdims=True), jnp.max(scores_txt, -1, keepdims=True)
    )
    exp_img = jnp.exp(scores_img - row_max)
    exp_txt = jnp.exp(scores_txt - row_max)
    total = jnp.sum(exp_img, -1, keepdims=True) + jnp.sum(exp_txt, -1, keepdims=True)
    weights_img = (exp_img / total).astype(jnp.bfloat16)
    weights_txt = (exp_txt / total).astype(jnp.bfloat16)
    mixed = jnp.einsum(
        "hqk,kf->hqf", weights_img, values_img, preferred_element_type=jnp.float32
    ) + jnp.einsum("hqk,kf->hqf", weights_txt, values_txt, preferred_element_type=jnp.float32)
    return jnp.sum(jnp.where(chosen[:, None, :], mixed, 0.0), 0).astype(jnp.bfloat16)


def reduce_rows(partial, parties):
    pieces = partial.reshape(parties, partial.shape[0] // parties, partial.shape[1])
    got = lax.all_to_all(pieces, "tp", split_axis=0, concat_axis=0, tiled=True)
    return jnp.sum(got.astype(jnp.float32), 0)


def spread(image_part, text_part, members):
    joined = jnp.concatenate([image_part, text_part], 0).transpose(1, 0, 2)
    widened = jnp.broadcast_to(joined[:, None], (joined.shape[0], members) + joined.shape[1:])
    return widened.reshape(joined.shape[0] * members, joined.shape[1], joined.shape[2])


def shards(
    img_hidden,
    txt_hidden,
    modulation,
    text_lengths,
    timestep_index,
    sigmas,
    latents,
    w_qkv,
    w_kv_text,
    w_out,
    w_up,
    w_down,
    w_final,
):
    img_slice = img_hidden.shape[1]
    requests = img_hidden.shape[2]
    model_width = img_hidden.shape[3]
    txt_slice = txt_hidden.shape[1]
    features = w_out.shape[0]
    members = lax.axis_size("seq") // requests
    parties = lax.axis_size("tp")
    portion = img_slice // parties
    rows_all = img_slice * requests
    adaptive = modulation[0].astype(jnp.float32)
    resident = img_hidden[0].astype(jnp.float32)
    lengths_all = text_lengths[0]
    normed = modulate(resident, adaptive[:, 0], adaptive[:, 1]).reshape(rows_all, model_width)
    projected = jnp.einsum(
        "nd,dkf->knf", normed, w_qkv, preferred_element_type=jnp.float32
    ).astype(jnp.bfloat16)
    queries = projected[0].reshape(img_slice, requests, features)
    keys_img = projected[1].reshape(img_slice, requests, features)
    vals_img = projected[2].reshape(img_slice, requests, features)
    text_in = modulate(txt_hidden[0].astype(jnp.float32), adaptive[:, 6], adaptive[:, 7]).reshape(
        txt_slice * requests, model_width
    )
    text_kv = jnp.einsum(
        "nd,dkf->knf", text_in, w_kv_text, preferred_element_type=jnp.float32
    ).astype(jnp.bfloat16)
    keys_txt = text_kv[0].reshape(txt_slice, requests, features)
    vals_txt = text_kv[1].reshape(txt_slice, requests, features)
    key_span = img_slice + txt_slice
    within = jnp.arange(key_span)
    senders = requests * members
    halves = members // 2
    query_share = img_slice // halves
    head_share = features // 2
    query_send = (
        queries.reshape(halves, query_share, requests, 2, head_share)
        .transpose(2, 0, 3, 1, 4)
        .reshape(senders, query_share, head_share)
    )
    def by_head_half(values, rows):
        return values.reshape(rows, requests, 2, head_share).transpose(1, 2, 0, 3)

    both = jnp.concatenate(
        [
            by_head_half(keys_img, img_slice),
            by_head_half(vals_img, img_slice),
            by_head_half(keys_txt, txt_slice),
            by_head_half(vals_txt, txt_slice),
        ],
        2,
    )
    kv_send = jnp.broadcast_to(
        both[:, None], (requests, halves, 2, 2 * key_span, head_share)
    ).reshape(senders, 2 * key_span, head_share)
    payload = jnp.concatenate([query_send, kv_send], 1)
    got = lax.all_to_all(payload, "seq", split_axis=0, concat_axis=0, tiled=True)
    cut = [query_share, img_slice, img_slice, txt_slice, txt_slice]
    edges = [sum(cut[:i]) for i in range(len(cut) + 1)]
    query_got, key_img_got, val_img_got, key_txt_got, val_txt_got = [
        got[:, edges[i] : edges[i + 1]].reshape(senders * cut[i], head_share)
        for i in range(len(cut))
    ]
    my_request = lax.axis_index("seq") // members
    length_now = jnp.sum(jnp.where(jnp.arange(requests) == my_request, lengths_all, 0))
    text_valid = jnp.arange(senders * txt_slice) < length_now
    answer = attend(query_got, key_img_got, val_img_got, key_txt_got, val_txt_got, text_valid)
    answer_back = lax.all_to_all(
        answer.reshape(senders, query_share, head_share),
        "seq",
        split_axis=0,
        concat_axis=0,
        tiled=True,
    )
    attn_rows = (
        answer_back.reshape(requests, halves, 2, query_share, head_share)
        .transpose(1, 3, 0, 2, 4)
        .reshape(rows_all, features)
    )
    tp_index = lax.axis_index("tp")
    resident_mine = lax.dynamic_slice_in_dim(resident, tp_index * portion, portion, 0)
    attn_part = jnp.dot(attn_rows, w_out, preferred_element_type=jnp.float32).astype(jnp.bfloat16)
    attn_mixed = reduce_rows(attn_part, parties).reshape(portion, requests, model_width)
    after_attn = resident_mine + adaptive[:, 2] * attn_mixed
    mlp_mine = modulate(after_attn, adaptive[:, 3], adaptive[:, 4])
    mlp_in = lax.all_gather(mlp_mine, "tp", axis=0, tiled=True).reshape(rows_all, model_width)
    hidden = jax.nn.gelu(
        jnp.dot(mlp_in, w_up, preferred_element_type=jnp.float32), approximate=True
    ).astype(jnp.bfloat16)
    mlp_part = jnp.dot(hidden, w_down, preferred_element_type=jnp.float32).astype(jnp.bfloat16)
    mlp_grown = reduce_rows(mlp_part, parties).reshape(portion, requests, model_width)
    after_mlp = after_attn + adaptive[:, 5] * mlp_grown
    head_in = modulate(after_mlp, adaptive[:, 8], adaptive[:, 9]).reshape(
        portion * requests, model_width
    )
    velocity_own = jnp.dot(head_in, w_final, preferred_element_type=jnp.float32).reshape(
        portion, requests, w_final.shape[1]
    )
    half_width = w_final.shape[1] // 2
    cfg_index = lax.axis_index("cfg")
    own_kept = lax.dynamic_slice_in_dim(velocity_own, cfg_index * half_width, half_width, 2)
    own_given = lax.dynamic_slice_in_dim(velocity_own, (1 - cfg_index) * half_width, half_width, 2)
    velocity_other = swapped(own_given, "cfg", 0)
    is_first = cfg_index == 0
    guided_cond = jnp.where(is_first, own_kept, velocity_other)
    guided_free = jnp.where(is_first, velocity_other, own_kept)
    velocity = guided_free + GUIDANCE * (guided_cond - guided_free)
    steps_all = jnp.arange(sigmas.shape[0], dtype=jnp.int32)
    sigma_now = jnp.sum(
        jnp.where(steps_all[None, :] == timestep_index[:, None], sigmas[None, :], 0.0), 1
    )
    sigma_after = jnp.sum(
        jnp.where(steps_all[None, :] == timestep_index[:, None] + 1, sigmas[None, :], 0.0), 1
    )
    latent_next = latents + (sigma_after - sigma_now)[None, :, None] * velocity
    return (velocity, latent_next)


def solution(mesh):
    return jax.shard_map(
        shards,
        mesh=mesh,
        in_specs=(
            P("cfg", "seq", None, None),
            P("cfg", "seq", None, None),
            P("cfg", None, None, None),
            P("cfg", None),
            P(),
            P(),
            P(("seq", "tp"), None, "cfg"),
            P(None, None, "tp"),
            P(None, None, "tp"),
            P("tp", None),
            P(None, "tp"),
            P("tp", None),
            P(),
        ),
        out_specs=(P(("seq", "tp"), None, "cfg"), P(("seq", "tp"), None, "cfg")),
        check_vma=False,
    )
```

```python
import math

import jax
import jax.numpy as jnp
from jax import lax
from jax.sharding import PartitionSpec as P

HEAD_DIM = 64


EPSILON = 1e-06
GUIDANCE = 7.0


def swapped(value, axis, apart):
    return lax.ppermute(value, axis, [(i, i ^ 1 << apart) for i in range(lax.axis_size(axis))])


def layer_norm(values):
    center = values - jnp.mean(values, -1, keepdims=True)
    return center * lax.rsqrt(jnp.mean(center * center, -1, keepdims=True) + EPSILON)


def modulate(values, shift_add, scale_mul):
    return (layer_norm(values) * (1.0 + scale_mul) + shift_add).astype(jnp.bfloat16)


def attend(queries, keys_in, values_in, key_valid):
    heads = queries.shape[2] // HEAD_DIM
    query_heads = queries.reshape(queries.shape[0], queries.shape[1], heads, HEAD_DIM)
    key_heads = keys_in.reshape(keys_in.shape[0], keys_in.shape[1], heads, HEAD_DIM)
    value_heads = values_in.reshape(values_in.shape[0], values_in.shape[1], heads, HEAD_DIM)
    scores = jnp.einsum(
        "qrhd,krhd->rhqk", query_heads, key_heads, preferred_element_type=jnp.float32
    ) * (1.0 / math.sqrt(HEAD_DIM))
    scores = jnp.where(key_valid[:, None, None, :], scores, -jnp.inf)
    row_max = jnp.max(scores, -1, keepdims=True)
    exp_scores = jnp.exp(scores - row_max)
    weights = (exp_scores / jnp.sum(exp_scores, -1, keepdims=True)).astype(jnp.bfloat16)
    result = jnp.einsum("rhqk,krhd->qrhd", weights, value_heads, preferred_element_type=jnp.float32)
    return result.astype(jnp.bfloat16).reshape(queries.shape)


def reduce_rows(partial, parties):
    pieces = partial.reshape(parties, partial.shape[0] // parties, partial.shape[1])
    got = lax.all_to_all(pieces, "tp", split_axis=0, concat_axis=0, tiled=True)
    return jnp.sum(got.astype(jnp.float32), 0)


def spread(image_part, text_part, members):
    joined = jnp.concatenate([image_part, text_part], 0).transpose(1, 0, 2)
    widened = jnp.broadcast_to(joined[:, None], (joined.shape[0], members) + joined.shape[1:])
    return widened.reshape(joined.shape[0] * members, joined.shape[1], joined.shape[2])


def shards(
    img_hidden,
    txt_hidden,
    modulation,
    text_lengths,
    timestep_index,
    sigmas,
    latents,
    w_qkv,
    w_kv_text,
    w_out,
    w_up,
    w_down,
    w_final,
):
    img_slice = img_hidden.shape[1]
    requests = img_hidden.shape[2]
    model_width = img_hidden.shape[3]
    txt_slice = txt_hidden.shape[1]
    features = w_out.shape[0]
    members = lax.axis_size("seq") // requests
    parties = lax.axis_size("tp")
    portion = img_slice // parties
    rows_all = img_slice * requests
    adaptive = modulation[0].astype(jnp.float32)
    resident = img_hidden[0].astype(jnp.float32)
    lengths_all = text_lengths[0]
    normed = modulate(resident, adaptive[:, 0], adaptive[:, 1]).reshape(rows_all, model_width)
    projected = jnp.dot(
        normed, w_qkv.reshape(model_width, 3 * features), preferred_element_type=jnp.float32
    ).astype(jnp.bfloat16)
    queries = projected[:, :features].reshape(img_slice, requests, features)
    keys_img = projected[:, features : 2 * features].reshape(img_slice, requests, features)
    vals_img = projected[:, 2 * features :].reshape(img_slice, requests, features)
    text_in = modulate(txt_hidden[0].astype(jnp.float32), adaptive[:, 6], adaptive[:, 7]).reshape(
        txt_slice * requests, model_width
    )
    text_kv = jnp.dot(
        text_in, w_kv_text.reshape(model_width, 2 * features), preferred_element_type=jnp.float32
    ).astype(jnp.bfloat16)
    keys_txt = text_kv[:, :features].reshape(txt_slice, requests, features)
    vals_txt = text_kv[:, features:].reshape(txt_slice, requests, features)
    key_span = img_slice + txt_slice
    within = jnp.arange(key_span)
    senders = requests * members
    halves = members // 2
    query_share = img_slice // halves
    head_share = features // 2
    query_send = (
        queries.reshape(halves, query_share, requests, 2, head_share)
        .transpose(2, 3, 0, 1, 4)
        .reshape(senders, query_share, head_share)
    )
    joined_k = jnp.concatenate([keys_img, keys_txt], 0).reshape(key_span, requests, 2, head_share)
    joined_v = jnp.concatenate([vals_img, vals_txt], 0).reshape(key_span, requests, 2, head_share)
    kv_send = (
        jnp.stack([joined_k, joined_v], 3)
        .transpose(1, 2, 3, 0, 4)
        .reshape(senders, key_span, head_share)
    )
    payload = jnp.concatenate([query_send, kv_send], 1)
    got = lax.all_to_all(payload, "seq", split_axis=0, concat_axis=0, tiled=True)
    query_got = got[:, :query_share]
    kv_mine = got[:, query_share:]
    kv_other = swapped(kv_mine, "seq", 0)
    first_core = lax.axis_index("seq") % 2 == 0
    key_got = jnp.where(first_core, kv_mine, kv_other)
    value_got = jnp.where(first_core, kv_other, kv_mine)
    my_request = lax.axis_index("seq") // members
    length_now = jnp.sum(jnp.where(jnp.arange(requests) == my_request, lengths_all, 0))
    text_slot = jnp.arange(senders)[:, None] * txt_slice + within[None, :] - img_slice
    key_valid = (within[None, :] < img_slice) | (text_slot < length_now)
    answer = attend(
        query_got.reshape(senders * query_share, 1, head_share),
        key_got.reshape(senders * key_span, 1, head_share),
        value_got.reshape(senders * key_span, 1, head_share),
        key_valid.reshape(1, senders * key_span),
    )
    answer_back = lax.all_to_all(
        answer.reshape(senders, query_share, head_share),
        "seq",
        split_axis=0,
        concat_axis=0,
        tiled=True,
    )
    attn_rows = (
        answer_back.reshape(requests, 2, halves, query_share, head_share)
        .transpose(2, 3, 0, 1, 4)
        .reshape(rows_all, features)
    )
    tp_index = lax.axis_index("tp")
    resident_mine = lax.dynamic_slice_in_dim(resident, tp_index * portion, portion, 0)
    attn_part = jnp.dot(attn_rows, w_out, preferred_element_type=jnp.float32).astype(jnp.bfloat16)
    attn_mixed = reduce_rows(attn_part, parties).reshape(portion, requests, model_width)
    after_attn = resident_mine + adaptive[:, 2] * attn_mixed
    mlp_mine = modulate(after_attn, adaptive[:, 3], adaptive[:, 4])
    mlp_in = lax.all_gather(mlp_mine, "tp", axis=0, tiled=True).reshape(rows_all, model_width)
    hidden = jax.nn.gelu(
        jnp.dot(mlp_in, w_up, preferred_element_type=jnp.float32), approximate=True
    ).astype(jnp.bfloat16)
    mlp_part = jnp.dot(hidden, w_down, preferred_element_type=jnp.float32).astype(jnp.bfloat16)
    mlp_grown = reduce_rows(mlp_part, parties).reshape(portion, requests, model_width)
    after_mlp = after_attn + adaptive[:, 5] * mlp_grown
    head_in = modulate(after_mlp, adaptive[:, 8], adaptive[:, 9]).reshape(
        portion * requests, model_width
    )
    velocity_own = jnp.dot(head_in, w_final, preferred_element_type=jnp.float32).reshape(
        portion, requests, w_final.shape[1]
    )
    half_width = w_final.shape[1] // 2
    cfg_index = lax.axis_index("cfg")
    own_kept = lax.dynamic_slice_in_dim(velocity_own, cfg_index * half_width, half_width, 2)
    own_given = lax.dynamic_slice_in_dim(velocity_own, (1 - cfg_index) * half_width, half_width, 2)
    velocity_other = swapped(own_given, "cfg", 0)
    is_first = cfg_index == 0
    guided_cond = jnp.where(is_first, own_kept, velocity_other)
    guided_free = jnp.where(is_first, velocity_other, own_kept)
    velocity = guided_free + GUIDANCE * (guided_cond - guided_free)
    steps_all = jnp.arange(sigmas.shape[0], dtype=jnp.int32)
    sigma_now = jnp.sum(
        jnp.where(steps_all[None, :] == timestep_index[:, None], sigmas[None, :], 0.0), 1
    )
    sigma_after = jnp.sum(
        jnp.where(steps_all[None, :] == timestep_index[:, None] + 1, sigmas[None, :], 0.0), 1
    )
    latent_next = latents + (sigma_after - sigma_now)[None, :, None] * velocity
    return (velocity, latent_next)


def solution(mesh):
    return jax.shard_map(
        shards,
        mesh=mesh,
        in_specs=(
            P("cfg", "seq", None, None),
            P("cfg", "seq", None, None),
            P("cfg", None, None, None),
            P("cfg", None),
            P(),
            P(),
            P(("seq", "tp"), None, "cfg"),
            P(None, None, "tp"),
            P(None, None, "tp"),
            P("tp", None),
            P(None, "tp"),
            P("tp", None),
            P(),
        ),
        out_specs=(P(("seq", "tp"), None, "cfg"), P(("seq", "tp"), None, "cfg")),
        check_vma=False,
    )
```

```python
import math

import jax
import jax.numpy as jnp
from jax import lax
from jax.experimental import pallas as pl
from jax.sharding import PartitionSpec as P

HEAD_DIM = 64


EPSILON = 1e-06
GUIDANCE = 7.0


def swapped(value, axis, apart):
    return lax.ppermute(value, axis, [(i, i ^ 1 << apart) for i in range(lax.axis_size(axis))])


def layer_norm(values):
    center = values - jnp.mean(values, -1, keepdims=True)
    return center * lax.rsqrt(jnp.mean(center * center, -1, keepdims=True) + EPSILON)


def modulate(values, shift_add, scale_mul):
    return (layer_norm(values) * (1.0 + scale_mul) + shift_add).astype(jnp.bfloat16)


def attention_kernel(q_ref, k_ref, v_ref, valid_ref, o_ref):
    queries = q_ref[...]
    keys = k_ref[...]
    values = v_ref[...]
    valid = valid_ref[...] > 0.5
    width = queries.shape[1]
    lane_head = lax.broadcasted_iota(jnp.int32, (1, width), 1) // HEAD_DIM
    result = jnp.zeros(o_ref.shape, jnp.float32)
    for head in range(width // HEAD_DIM):
        chosen = lane_head == head
        query_head = jnp.where(chosen, queries, jnp.zeros_like(queries))
        scores = lax.dot_general(
            query_head, keys, (((1,), (1,)), ((), ())), preferred_element_type=jnp.float32
        ) * (1.0 / math.sqrt(HEAD_DIM))
        scores = jnp.where(valid, scores, -jnp.inf)
        row_max = jnp.max(scores, axis=1, keepdims=True)
        exp_scores = jnp.exp(scores - row_max)
        total = jnp.sum(exp_scores, axis=1, keepdims=True)
        weights = (exp_scores / total).astype(jnp.bfloat16)
        mixed = jnp.dot(weights, values, preferred_element_type=jnp.float32)
        result = jnp.where(chosen, mixed, result)
    o_ref[...] = result.astype(o_ref.dtype)

def attend_kernel(queries, keys, values, valid):
    return pl.pallas_call(
        attention_kernel,
        out_shape=jax.ShapeDtypeStruct(queries.shape, jnp.bfloat16),
    )(queries, keys, values, valid)


def reduce_rows(partial, parties):
    pieces = partial.reshape(parties, partial.shape[0] // parties, partial.shape[1])
    got = lax.all_to_all(pieces, "tp", split_axis=0, concat_axis=0, tiled=True)
    return jnp.sum(got.astype(jnp.float32), 0)


def shards(
    img_hidden,
    txt_hidden,
    modulation,
    text_lengths,
    timestep_index,
    sigmas,
    latents,
    w_qkv,
    w_kv_text,
    w_out,
    w_up,
    w_down,
    w_final,
):
    img_slice = img_hidden.shape[1]
    requests = img_hidden.shape[2]
    model_width = img_hidden.shape[3]
    txt_slice = txt_hidden.shape[1]
    features = w_out.shape[0]
    members = lax.axis_size("seq") // requests
    parties = lax.axis_size("tp")
    portion = img_slice // parties
    rows_all = img_slice * requests
    adaptive = modulation[0].astype(jnp.float32)
    resident = img_hidden[0].astype(jnp.float32)
    lengths_all = text_lengths[0]
    normed = modulate(resident, adaptive[:, 0], adaptive[:, 1]).reshape(rows_all, model_width)
    projected = jnp.dot(
        normed, w_qkv.reshape(model_width, 3 * features), preferred_element_type=jnp.float32
    ).astype(jnp.bfloat16)
    queries = projected[:, :features].reshape(img_slice, requests, features)
    keys_img = projected[:, features : 2 * features].reshape(img_slice, requests, features)
    vals_img = projected[:, 2 * features :].reshape(img_slice, requests, features)
    text_in = modulate(txt_hidden[0].astype(jnp.float32), adaptive[:, 6], adaptive[:, 7]).reshape(
        txt_slice * requests, model_width
    )
    text_kv = jnp.dot(
        text_in, w_kv_text.reshape(model_width, 2 * features), preferred_element_type=jnp.float32
    ).astype(jnp.bfloat16)
    keys_txt = text_kv[:, :features].reshape(txt_slice, requests, features)
    vals_txt = text_kv[:, features:].reshape(txt_slice, requests, features)
    key_span = img_slice + txt_slice
    senders = requests * members
    halves = members // 2
    query_share = img_slice // halves
    head_share = features // 2
    query_send = (
        queries.reshape(halves, query_share, requests, 2, head_share)
        .transpose(2, 3, 0, 1, 4)
        .reshape(senders, query_share, head_share)
    )
    joined_k = jnp.concatenate([keys_img, keys_txt], 0).reshape(key_span, requests, 2, head_share)
    joined_v = jnp.concatenate([vals_img, vals_txt], 0).reshape(key_span, requests, 2, head_share)
    kv_send = (
        jnp.stack([joined_k, joined_v], 3)
        .transpose(1, 2, 3, 0, 4)
        .reshape(senders, key_span, head_share)
    )
    payload = jnp.concatenate([query_send, kv_send], 1)
    got = lax.all_to_all(payload, "seq", split_axis=0, concat_axis=0, tiled=True)
    query_got = got[:, :query_share]
    kv_mine = got[:, query_share:]
    kv_other = swapped(kv_mine, "seq", 0)
    first_core = lax.axis_index("seq") % 2 == 0
    key_got = jnp.where(first_core, kv_mine, kv_other)
    value_got = jnp.where(first_core, kv_other, kv_mine)
    my_request = lax.axis_index("seq") // members
    length_now = jnp.sum(jnp.where(jnp.arange(requests) == my_request, lengths_all, 0))
    padded_span = -(-key_span // 8) * 8
    slot = jnp.arange(padded_span)
    text_slot = jnp.arange(senders)[:, None] * txt_slice + slot[None, :] - img_slice
    key_valid = (slot[None, :] < img_slice) | ((slot[None, :] < key_span) & (text_slot < length_now))

    def padded(block):
        return jnp.pad(block, ((0, 0), (0, padded_span - key_span), (0, 0))).reshape(
            senders * padded_span, head_share
        )

    answer = attend_kernel(
        query_got.reshape(senders * query_share, head_share),
        padded(key_got),
        padded(value_got),
        key_valid.astype(jnp.float32).reshape(1, senders * padded_span),
    )
    answer_back = lax.all_to_all(
        answer.reshape(senders, query_share, head_share),
        "seq",
        split_axis=0,
        concat_axis=0,
        tiled=True,
    )
    attn_rows = (
        answer_back.reshape(requests, 2, halves, query_share, head_share)
        .transpose(2, 3, 0, 1, 4)
        .reshape(rows_all, features)
    )
    tp_index = lax.axis_index("tp")
    resident_mine = lax.dynamic_slice_in_dim(resident, tp_index * portion, portion, 0)
    attn_part = jnp.dot(attn_rows, w_out, preferred_element_type=jnp.float32).astype(jnp.bfloat16)
    attn_mixed = reduce_rows(attn_part, parties).reshape(portion, requests, model_width)
    after_attn = resident_mine + adaptive[:, 2] * attn_mixed
    mlp_mine = modulate(after_attn, adaptive[:, 3], adaptive[:, 4])
    mlp_in = lax.all_gather(mlp_mine, "tp", axis=0, tiled=True).reshape(rows_all, model_width)
    hidden = jax.nn.gelu(
        jnp.dot(mlp_in, w_up, preferred_element_type=jnp.float32), approximate=True
    ).astype(jnp.bfloat16)
    mlp_part = jnp.dot(hidden, w_down, preferred_element_type=jnp.float32).astype(jnp.bfloat16)
    mlp_grown = reduce_rows(mlp_part, parties).reshape(portion, requests, model_width)
    after_mlp = after_attn + adaptive[:, 5] * mlp_grown
    head_in = modulate(after_mlp, adaptive[:, 8], adaptive[:, 9]).reshape(
        portion * requests, model_width
    )
    velocity_own = jnp.dot(head_in, w_final, preferred_element_type=jnp.float32).reshape(
        portion, requests, w_final.shape[1]
    )
    half_width = w_final.shape[1] // 2
    cfg_index = lax.axis_index("cfg")
    own_kept = lax.dynamic_slice_in_dim(velocity_own, cfg_index * half_width, half_width, 2)
    own_given = lax.dynamic_slice_in_dim(velocity_own, (1 - cfg_index) * half_width, half_width, 2)
    velocity_other = swapped(own_given, "cfg", 0)
    is_first = cfg_index == 0
    guided_cond = jnp.where(is_first, own_kept, velocity_other)
    guided_free = jnp.where(is_first, velocity_other, own_kept)
    velocity = guided_free + GUIDANCE * (guided_cond - guided_free)
    steps_all = jnp.arange(sigmas.shape[0], dtype=jnp.int32)
    sigma_now = jnp.sum(
        jnp.where(steps_all[None, :] == timestep_index[:, None], sigmas[None, :], 0.0), 1
    )
    sigma_after = jnp.sum(
        jnp.where(steps_all[None, :] == timestep_index[:, None] + 1, sigmas[None, :], 0.0), 1
    )
    latent_next = latents + (sigma_after - sigma_now)[None, :, None] * velocity
    return (velocity, latent_next)


def solution(mesh):
    return jax.shard_map(
        shards,
        mesh=mesh,
        in_specs=(
            P("cfg", "seq", None, None),
            P("cfg", "seq", None, None),
            P("cfg", None, None, None),
            P("cfg", None),
            P(),
            P(),
            P(("seq", "tp"), None, "cfg"),
            P(None, None, "tp"),
            P(None, None, "tp"),
            P("tp", None),
            P(None, "tp"),
            P("tp", None),
            P(),
        ),
        out_specs=(P(("seq", "tp"), None, "cfg"), P(("seq", "tp"), None, "cfg")),
        check_vma=False,
    )
```

```python
import math

import jax
import jax.numpy as jnp
from jax import lax
from jax.experimental import pallas as pl
from jax.sharding import PartitionSpec as P

HEAD_DIM = 64


EPSILON = 1e-06
GUIDANCE = 7.0


def swapped(value, axis, apart):
    return lax.ppermute(value, axis, [(i, i ^ 1 << apart) for i in range(lax.axis_size(axis))])


def layer_norm(values):
    center = values - jnp.mean(values, -1, keepdims=True)
    return center * lax.rsqrt(jnp.mean(center * center, -1, keepdims=True) + EPSILON)


def modulate(values, shift_add, scale_mul):
    return (layer_norm(values) * (1.0 + scale_mul) + shift_add).astype(jnp.bfloat16)


def attention_kernel(q_ref, k_ref, v_ref, valid_ref, o_ref):
    queries = q_ref[...]
    keys = k_ref[...]
    values = v_ref[...]
    valid = valid_ref[...] > 0.5
    width = queries.shape[1]
    lane_head = lax.broadcasted_iota(jnp.int32, (1, width), 1) // HEAD_DIM
    result = jnp.zeros(o_ref.shape, jnp.float32)
    for head in range(width // HEAD_DIM):
        chosen = lane_head == head
        query_head = jnp.where(chosen, queries, jnp.zeros_like(queries))
        scores = lax.dot_general(
            query_head, keys, (((1,), (1,)), ((), ())), preferred_element_type=jnp.float32
        ) * (1.0 / math.sqrt(HEAD_DIM))
        scores = jnp.where(valid, scores, -jnp.inf)
        row_max = jnp.max(scores, axis=1, keepdims=True)
        exp_scores = jnp.exp(scores - row_max)
        total = jnp.sum(exp_scores, axis=1, keepdims=True)
        weights = (exp_scores / total).astype(jnp.bfloat16)
        mixed = jnp.dot(weights, values, preferred_element_type=jnp.float32)
        result = jnp.where(chosen, mixed, result)
    o_ref[...] = result.astype(o_ref.dtype)

def attend_kernel(queries, keys, values, valid):
    return pl.pallas_call(
        attention_kernel,
        out_shape=jax.ShapeDtypeStruct(queries.shape, jnp.bfloat16),
    )(queries, keys, values, valid)


def shifted(value, axis, step):
    size = lax.axis_size(axis)
    return lax.ppermute(value, axis, [(i, (i + step) % size) for i in range(size)])


def reduce_rows(partial, parties):
    pieces = partial.reshape(parties, partial.shape[0] // parties, partial.shape[1])
    me = lax.axis_index("tp")
    total = lax.dynamic_index_in_dim(pieces, me, 0, False).astype(jnp.float32)
    for step in range(1, parties):
        sent = lax.dynamic_index_in_dim(pieces, (me + step) % parties, 0, False)
        total = total + shifted(sent, "tp", step).astype(jnp.float32)
    return total


def gather_blocks(block, parties):
    return jnp.stack([block] + [shifted(block, "tp", step) for step in range(1, parties)], 0)


def return_blocks(partial, parties):
    pieces = partial.reshape(parties, partial.shape[0] // parties, partial.shape[1])
    total = pieces[0].astype(jnp.float32)
    for step in range(1, parties):
        total = total + shifted(pieces[step], "tp", -step).astype(jnp.float32)
    return total


def shards(
    img_hidden,
    txt_hidden,
    modulation,
    text_lengths,
    timestep_index,
    sigmas,
    latents,
    w_qkv,
    w_kv_text,
    w_out,
    w_up,
    w_down,
    w_final,
):
    img_slice = img_hidden.shape[1]
    requests = img_hidden.shape[2]
    model_width = img_hidden.shape[3]
    txt_slice = txt_hidden.shape[1]
    features = w_out.shape[0]
    members = lax.axis_size("seq") // requests
    parties = lax.axis_size("tp")
    portion = img_slice // parties
    rows_all = img_slice * requests
    adaptive = modulation[0].astype(jnp.float32)
    resident = img_hidden[0].astype(jnp.float32)
    lengths_all = text_lengths[0]
    normed = modulate(resident, adaptive[:, 0], adaptive[:, 1]).reshape(rows_all, model_width)
    projected = jnp.dot(
        normed, w_qkv.reshape(model_width, 3 * features), preferred_element_type=jnp.float32
    ).astype(jnp.bfloat16)
    queries = projected[:, :features].reshape(img_slice, requests, features)
    keys_img = projected[:, features : 2 * features].reshape(img_slice, requests, features)
    vals_img = projected[:, 2 * features :].reshape(img_slice, requests, features)
    text_in = modulate(txt_hidden[0].astype(jnp.float32), adaptive[:, 6], adaptive[:, 7]).reshape(
        txt_slice * requests, model_width
    )
    text_kv = jnp.dot(
        text_in, w_kv_text.reshape(model_width, 2 * features), preferred_element_type=jnp.float32
    ).astype(jnp.bfloat16)
    keys_txt = text_kv[:, :features].reshape(txt_slice, requests, features)
    vals_txt = text_kv[:, features:].reshape(txt_slice, requests, features)
    key_span = img_slice + txt_slice
    senders = requests * members
    halves = members // 2
    query_share = img_slice // halves
    head_share = features // 2
    query_send = (
        queries.reshape(halves, query_share, requests, 2, head_share)
        .transpose(2, 3, 0, 1, 4)
        .reshape(senders, query_share, head_share)
    )
    joined_k = jnp.concatenate([keys_img, keys_txt], 0).reshape(key_span, requests, 2, head_share)
    joined_v = jnp.concatenate([vals_img, vals_txt], 0).reshape(key_span, requests, 2, head_share)
    kv_send = (
        jnp.stack([joined_k, joined_v], 3)
        .transpose(1, 2, 3, 0, 4)
        .reshape(senders, key_span, head_share)
    )
    payload = jnp.concatenate([query_send, kv_send], 1)
    got = lax.all_to_all(payload, "seq", split_axis=0, concat_axis=0, tiled=True)
    query_got = got[:, :query_share]
    kv_mine = got[:, query_share:]
    kv_other = swapped(kv_mine, "seq", 0)
    first_core = lax.axis_index("seq") % 2 == 0
    key_got = jnp.where(first_core, kv_mine, kv_other)
    value_got = jnp.where(first_core, kv_other, kv_mine)
    my_request = lax.axis_index("seq") // members
    length_now = jnp.sum(jnp.where(jnp.arange(requests) == my_request, lengths_all, 0))
    padded_span = -(-key_span // 8) * 8
    slot = jnp.arange(padded_span)
    text_slot = jnp.arange(senders)[:, None] * txt_slice + slot[None, :] - img_slice
    key_valid = (slot[None, :] < img_slice) | ((slot[None, :] < key_span) & (text_slot < length_now))

    def padded(block):
        return jnp.pad(block, ((0, 0), (0, padded_span - key_span), (0, 0))).reshape(
            senders * padded_span, head_share
        )

    answer = attend_kernel(
        query_got.reshape(senders * query_share, head_share),
        padded(key_got),
        padded(value_got),
        key_valid.astype(jnp.float32).reshape(1, senders * padded_span),
    )
    answer_back = lax.all_to_all(
        answer.reshape(senders, query_share, head_share),
        "seq",
        split_axis=0,
        concat_axis=0,
        tiled=True,
    )
    attn_rows = (
        answer_back.reshape(requests, 2, halves, query_share, head_share)
        .transpose(2, 3, 0, 1, 4)
        .reshape(rows_all, features)
    )
    tp_index = lax.axis_index("tp")
    resident_mine = lax.dynamic_slice_in_dim(resident, tp_index * portion, portion, 0)
    attn_part = jnp.dot(attn_rows, w_out, preferred_element_type=jnp.float32).astype(jnp.bfloat16)
    attn_mixed = reduce_rows(attn_part, parties).reshape(portion, requests, model_width)
    after_attn = resident_mine + adaptive[:, 2] * attn_mixed
    mlp_mine = modulate(after_attn, adaptive[:, 3], adaptive[:, 4])
    mlp_in = gather_blocks(mlp_mine, parties).reshape(rows_all, model_width)
    hidden = jax.nn.gelu(
        jnp.dot(mlp_in, w_up, preferred_element_type=jnp.float32), approximate=True
    ).astype(jnp.bfloat16)
    mlp_part = jnp.dot(hidden, w_down, preferred_element_type=jnp.float32).astype(jnp.bfloat16)
    mlp_grown = return_blocks(mlp_part, parties).reshape(portion, requests, model_width)
    after_mlp = after_attn + adaptive[:, 5] * mlp_grown
    head_in = modulate(after_mlp, adaptive[:, 8], adaptive[:, 9]).reshape(
        portion * requests, model_width
    )
    velocity_own = jnp.dot(head_in, w_final, preferred_element_type=jnp.float32).reshape(
        portion, requests, w_final.shape[1]
    )
    half_width = w_final.shape[1] // 2
    cfg_index = lax.axis_index("cfg")
    own_kept = lax.dynamic_slice_in_dim(velocity_own, cfg_index * half_width, half_width, 2)
    own_given = lax.dynamic_slice_in_dim(velocity_own, (1 - cfg_index) * half_width, half_width, 2)
    velocity_other = swapped(own_given, "cfg", 0)
    is_first = cfg_index == 0
    guided_cond = jnp.where(is_first, own_kept, velocity_other)
    guided_free = jnp.where(is_first, velocity_other, own_kept)
    velocity = guided_free + GUIDANCE * (guided_cond - guided_free)
    steps_all = jnp.arange(sigmas.shape[0], dtype=jnp.int32)
    sigma_now = jnp.sum(
        jnp.where(steps_all[None, :] == timestep_index[:, None], sigmas[None, :], 0.0), 1
    )
    sigma_after = jnp.sum(
        jnp.where(steps_all[None, :] == timestep_index[:, None] + 1, sigmas[None, :], 0.0), 1
    )
    latent_next = latents + (sigma_after - sigma_now)[None, :, None] * velocity
    return (velocity, latent_next)


def solution(mesh):
    return jax.shard_map(
        shards,
        mesh=mesh,
        in_specs=(
            P("cfg", "seq", None, None),
            P("cfg", "seq", None, None),
            P("cfg", None, None, None),
            P("cfg", None),
            P(),
            P(),
            P(("seq", "tp"), None, "cfg"),
            P(None, None, "tp"),
            P(None, None, "tp"),
            P("tp", None),
            P(None, "tp"),
            P("tp", None),
            P(),
        ),
        out_specs=(P(("seq", "tp"), None, "cfg"), P(("seq", "tp"), None, "cfg")),
        check_vma=False,
    )
```

```python
import math

import jax
import jax.numpy as jnp
from jax import lax
from jax.experimental import pallas as pl
from jax.sharding import PartitionSpec as P

HEAD_DIM = 64


EPSILON = 1e-06
GUIDANCE = 7.0


def swapped(value, axis, apart):
    return lax.ppermute(value, axis, [(i, i ^ 1 << apart) for i in range(lax.axis_size(axis))])


def layer_norm(values):
    center = values - jnp.mean(values, -1, keepdims=True)
    return center * lax.rsqrt(jnp.mean(center * center, -1, keepdims=True) + EPSILON)


def modulate(values, shift_add, scale_mul):
    return (layer_norm(values) * (1.0 + scale_mul) + shift_add).astype(jnp.bfloat16)


def attention_kernel(q_ref, k_ref, v_ref, valid_ref, o_ref):
    queries = q_ref[...]
    keys = k_ref[...]
    values = v_ref[...]
    valid = valid_ref[...] > 0.5
    width = queries.shape[1]
    lane_head = lax.broadcasted_iota(jnp.int32, (1, width), 1) // HEAD_DIM
    result = jnp.zeros(o_ref.shape, jnp.float32)
    for head in range(width // HEAD_DIM):
        chosen = lane_head == head
        query_head = jnp.where(chosen, queries, jnp.zeros_like(queries))
        scores = lax.dot_general(
            query_head, keys, (((1,), (1,)), ((), ())), preferred_element_type=jnp.float32
        ) * (1.0 / math.sqrt(HEAD_DIM))
        scores = jnp.where(valid, scores, -jnp.inf)
        row_max = jnp.max(scores, axis=1, keepdims=True)
        exp_scores = jnp.exp(scores - row_max)
        total = jnp.sum(exp_scores, axis=1, keepdims=True)
        weights = (exp_scores / total).astype(jnp.bfloat16)
        mixed = jnp.dot(weights, values, preferred_element_type=jnp.float32)
        result = jnp.where(chosen, mixed, result)
    o_ref[...] = result.astype(o_ref.dtype)

def attend_kernel(queries, keys, values, valid):
    return pl.pallas_call(
        attention_kernel,
        out_shape=jax.ShapeDtypeStruct(queries.shape, jnp.bfloat16),
    )(queries, keys, values, valid)


def reduce_rows(partial, parties):
    pieces = partial.reshape(parties, partial.shape[0] // parties, partial.shape[1])
    got = lax.all_to_all(pieces, "tp", split_axis=0, concat_axis=0, tiled=True)
    return jnp.sum(got.astype(jnp.float32), 0)


def shards(
    img_hidden,
    txt_hidden,
    modulation,
    text_lengths,
    timestep_index,
    sigmas,
    latents,
    w_qkv,
    w_kv_text,
    w_out,
    w_up,
    w_down,
    w_final,
):
    img_slice = img_hidden.shape[1]
    requests = img_hidden.shape[2]
    model_width = img_hidden.shape[3]
    txt_slice = txt_hidden.shape[1]
    features = w_out.shape[0]
    members = lax.axis_size("seq") // requests
    parties = lax.axis_size("tp")
    portion = img_slice // parties
    rows_all = img_slice * requests
    adaptive = modulation[0].astype(jnp.float32)
    resident = img_hidden[0].astype(jnp.float32)
    lengths_all = text_lengths[0]
    normed = modulate(resident, adaptive[:, 0], adaptive[:, 1]).reshape(rows_all, model_width)
    projected = jnp.einsum(
        "nd,dkf->knf", normed, w_qkv, preferred_element_type=jnp.float32
    ).astype(jnp.bfloat16)
    queries = projected[0].reshape(img_slice, requests, features)
    keys_img = projected[1].reshape(img_slice, requests, features)
    vals_img = projected[2].reshape(img_slice, requests, features)
    text_in = modulate(txt_hidden[0].astype(jnp.float32), adaptive[:, 6], adaptive[:, 7]).reshape(
        txt_slice * requests, model_width
    )
    text_kv = jnp.einsum(
        "nd,dkf->knf", text_in, w_kv_text, preferred_element_type=jnp.float32
    ).astype(jnp.bfloat16)
    keys_txt = text_kv[0].reshape(txt_slice, requests, features)
    vals_txt = text_kv[1].reshape(txt_slice, requests, features)
    key_span = img_slice + txt_slice
    senders = requests * members
    halves = members // 2
    query_share = img_slice // halves
    head_share = features // 2
    query_send = (
        queries.reshape(halves, query_share, requests, 2, head_share)
        .transpose(2, 3, 0, 1, 4)
        .reshape(senders, query_share, head_share)
    )
    joined_k = jnp.concatenate([keys_img, keys_txt], 0).reshape(key_span, requests, 2, head_share)
    joined_v = jnp.concatenate([vals_img, vals_txt], 0).reshape(key_span, requests, 2, head_share)
    kv_send = (
        jnp.stack([joined_k, joined_v], 3)
        .transpose(1, 2, 3, 0, 4)
        .reshape(senders, key_span, head_share)
    )
    payload = jnp.concatenate([query_send, kv_send], 1)
    got = lax.all_to_all(payload, "seq", split_axis=0, concat_axis=0, tiled=True)
    query_got = got[:, :query_share]
    kv_mine = got[:, query_share:]
    kv_other = swapped(kv_mine, "seq", 0)
    first_core = lax.axis_index("seq") % 2 == 0
    key_got = jnp.where(first_core, kv_mine, kv_other)
    value_got = jnp.where(first_core, kv_other, kv_mine)
    my_request = lax.axis_index("seq") // members
    length_now = jnp.sum(jnp.where(jnp.arange(requests) == my_request, lengths_all, 0))
    padded_span = -(-key_span // 8) * 8
    slot = jnp.arange(padded_span)
    text_slot = jnp.arange(senders)[:, None] * txt_slice + slot[None, :] - img_slice
    key_valid = (slot[None, :] < img_slice) | ((slot[None, :] < key_span) & (text_slot < length_now))

    def padded(block):
        return jnp.pad(block, ((0, 0), (0, padded_span - key_span), (0, 0))).reshape(
            senders * padded_span, head_share
        )

    answer = attend_kernel(
        query_got.reshape(senders * query_share, head_share),
        padded(key_got),
        padded(value_got),
        key_valid.astype(jnp.float32).reshape(1, senders * padded_span),
    )
    answer_back = lax.all_to_all(
        answer.reshape(senders, query_share, head_share),
        "seq",
        split_axis=0,
        concat_axis=0,
        tiled=True,
    )
    attn_rows = (
        answer_back.reshape(requests, 2, halves, query_share, head_share)
        .transpose(2, 3, 0, 1, 4)
        .reshape(rows_all, features)
    )
    tp_index = lax.axis_index("tp")
    resident_mine = lax.dynamic_slice_in_dim(resident, tp_index * portion, portion, 0)
    attn_part = jnp.dot(attn_rows, w_out, preferred_element_type=jnp.float32).astype(jnp.bfloat16)
    attn_mixed = reduce_rows(attn_part, parties).reshape(portion, requests, model_width)
    after_attn = resident_mine + adaptive[:, 2] * attn_mixed
    mlp_mine = modulate(after_attn, adaptive[:, 3], adaptive[:, 4])
    mlp_in = lax.all_gather(mlp_mine, "tp", axis=0, tiled=True).reshape(rows_all, model_width)
    hidden = jax.nn.gelu(
        jnp.dot(mlp_in, w_up, preferred_element_type=jnp.float32), approximate=True
    ).astype(jnp.bfloat16)
    mlp_part = jnp.dot(hidden, w_down, preferred_element_type=jnp.float32).astype(jnp.bfloat16)
    mlp_grown = reduce_rows(mlp_part, parties).reshape(portion, requests, model_width)
    after_mlp = after_attn + adaptive[:, 5] * mlp_grown
    head_in = modulate(after_mlp, adaptive[:, 8], adaptive[:, 9]).reshape(
        portion * requests, model_width
    )
    velocity_own = jnp.dot(head_in, w_final, preferred_element_type=jnp.float32).reshape(
        portion, requests, w_final.shape[1]
    )
    half_width = w_final.shape[1] // 2
    cfg_index = lax.axis_index("cfg")
    own_kept = lax.dynamic_slice_in_dim(velocity_own, cfg_index * half_width, half_width, 2)
    own_given = lax.dynamic_slice_in_dim(velocity_own, (1 - cfg_index) * half_width, half_width, 2)
    velocity_other = swapped(own_given, "cfg", 0)
    is_first = cfg_index == 0
    guided_cond = jnp.where(is_first, own_kept, velocity_other)
    guided_free = jnp.where(is_first, velocity_other, own_kept)
    velocity = guided_free + GUIDANCE * (guided_cond - guided_free)
    steps_all = jnp.arange(sigmas.shape[0], dtype=jnp.int32)
    sigma_now = jnp.sum(
        jnp.where(steps_all[None, :] == timestep_index[:, None], sigmas[None, :], 0.0), 1
    )
    sigma_after = jnp.sum(
        jnp.where(steps_all[None, :] == timestep_index[:, None] + 1, sigmas[None, :], 0.0), 1
    )
    latent_next = latents + (sigma_after - sigma_now)[None, :, None] * velocity
    return (velocity, latent_next)


def solution(mesh):
    return jax.shard_map(
        shards,
        mesh=mesh,
        in_specs=(
            P("cfg", "seq", None, None),
            P("cfg", "seq", None, None),
            P("cfg", None, None, None),
            P("cfg", None),
            P(),
            P(),
            P(("seq", "tp"), None, "cfg"),
            P(None, None, "tp"),
            P(None, None, "tp"),
            P("tp", None),
            P(None, "tp"),
            P("tp", None),
            P(),
        ),
        out_specs=(P(("seq", "tp"), None, "cfg"), P(("seq", "tp"), None, "cfg")),
        check_vma=False,
    )
```

```python
import math

import jax
import jax.numpy as jnp
from jax import lax
from jax.experimental import pallas as pl
from jax.sharding import PartitionSpec as P

HEAD_DIM = 64


EPSILON = 1e-06
GUIDANCE = 7.0


def swapped(value, axis, apart):
    return lax.ppermute(value, axis, [(i, i ^ 1 << apart) for i in range(lax.axis_size(axis))])


def layer_norm(values):
    center = values - jnp.mean(values, -1, keepdims=True)
    return center * lax.rsqrt(jnp.mean(center * center, -1, keepdims=True) + EPSILON)


def modulate(values, shift_add, scale_mul):
    return (layer_norm(values) * (1.0 + scale_mul) + shift_add).astype(jnp.bfloat16)


def attention_kernel(q_ref, k_ref, v_ref, valid_ref, o_ref):
    queries = q_ref[...]
    keys = k_ref[...]
    values = v_ref[...]
    valid = valid_ref[...] > 0.5
    width = queries.shape[1]
    lane_head = lax.broadcasted_iota(jnp.int32, (1, width), 1) // HEAD_DIM
    result = jnp.zeros(o_ref.shape, jnp.float32)
    for head in range(width // HEAD_DIM):
        chosen = lane_head == head
        query_head = jnp.where(chosen, queries, jnp.zeros_like(queries))
        scores = lax.dot_general(
            query_head, keys, (((1,), (1,)), ((), ())), preferred_element_type=jnp.float32
        ) * (1.0 / math.sqrt(HEAD_DIM))
        scores = jnp.where(valid, scores, -jnp.inf)
        row_max = jnp.max(scores, axis=1, keepdims=True)
        exp_scores = jnp.exp(scores - row_max)
        total = jnp.sum(exp_scores, axis=1, keepdims=True)
        weights = (exp_scores / total).astype(jnp.bfloat16)
        mixed = jnp.dot(weights, values, preferred_element_type=jnp.float32)
        result = jnp.where(chosen, mixed, result)
    o_ref[...] = result.astype(o_ref.dtype)

def attend_kernel(queries, keys, values, valid):
    return pl.pallas_call(
        attention_kernel,
        out_shape=jax.ShapeDtypeStruct(queries.shape, jnp.bfloat16),
    )(queries, keys, values, valid)


def reduce_rows(partial, parties):
    pieces = partial.reshape(parties, partial.shape[0] // parties, partial.shape[1])
    got = lax.all_to_all(pieces, "tp", split_axis=0, concat_axis=0, tiled=True)
    return jnp.sum(got.astype(jnp.float32), 0)


def shards(
    img_hidden,
    txt_hidden,
    modulation,
    text_lengths,
    timestep_index,
    sigmas,
    latents,
    w_qkv,
    w_kv_text,
    w_out,
    w_up,
    w_down,
    w_final,
):
    img_slice = img_hidden.shape[1]
    requests = img_hidden.shape[2]
    model_width = img_hidden.shape[3]
    txt_slice = txt_hidden.shape[1]
    features = w_out.shape[0]
    members = lax.axis_size("seq") // requests
    parties = lax.axis_size("tp")
    portion = img_slice // parties
    rows_all = img_slice * requests
    adaptive = modulation[0].astype(jnp.float32)
    resident = img_hidden[0].astype(jnp.float32)
    lengths_all = text_lengths[0]
    normed = modulate(resident, adaptive[:, 0], adaptive[:, 1]).reshape(rows_all, model_width)
    queries, keys_img, vals_img = [
        jnp.dot(normed, w_qkv[:, part], preferred_element_type=jnp.float32)
        .astype(jnp.bfloat16)
        .reshape(img_slice, requests, features)
        for part in range(3)
    ]
    text_in = modulate(txt_hidden[0].astype(jnp.float32), adaptive[:, 6], adaptive[:, 7]).reshape(
        txt_slice * requests, model_width
    )
    text_kv = jnp.dot(
        text_in, w_kv_text.reshape(model_width, 2 * features), preferred_element_type=jnp.float32
    ).astype(jnp.bfloat16)
    keys_txt = text_kv[:, :features].reshape(txt_slice, requests, features)
    vals_txt = text_kv[:, features:].reshape(txt_slice, requests, features)
    key_span = img_slice + txt_slice
    senders = requests * members
    halves = members // 2
    query_share = img_slice // halves
    head_share = features // 2
    query_send = (
        queries.reshape(halves, query_share, requests, 2, head_share)
        .transpose(2, 3, 0, 1, 4)
        .reshape(senders, query_share, head_share)
    )
    joined_k = jnp.concatenate([keys_img, keys_txt], 0).reshape(key_span, requests, 2, head_share)
    joined_v = jnp.concatenate([vals_img, vals_txt], 0).reshape(key_span, requests, 2, head_share)
    kv_send = (
        jnp.stack([joined_k, joined_v], 3)
        .transpose(1, 2, 3, 0, 4)
        .reshape(senders, key_span, head_share)
    )
    payload = jnp.concatenate([query_send, kv_send], 1)
    got = lax.all_to_all(payload, "seq", split_axis=0, concat_axis=0, tiled=True)
    query_got = got[:, :query_share]
    kv_mine = got[:, query_share:]
    kv_other = swapped(kv_mine, "seq", 0)
    first_core = lax.axis_index("seq") % 2 == 0
    key_got = jnp.where(first_core, kv_mine, kv_other)
    value_got = jnp.where(first_core, kv_other, kv_mine)
    my_request = lax.axis_index("seq") // members
    length_now = jnp.sum(jnp.where(jnp.arange(requests) == my_request, lengths_all, 0))
    padded_span = -(-key_span // 8) * 8
    slot = jnp.arange(padded_span)
    text_slot = jnp.arange(senders)[:, None] * txt_slice + slot[None, :] - img_slice
    key_valid = (slot[None, :] < img_slice) | ((slot[None, :] < key_span) & (text_slot < length_now))

    def padded(block):
        return jnp.pad(block, ((0, 0), (0, padded_span - key_span), (0, 0))).reshape(
            senders * padded_span, head_share
        )

    answer = attend_kernel(
        query_got.reshape(senders * query_share, head_share),
        padded(key_got),
        padded(value_got),
        key_valid.astype(jnp.float32).reshape(1, senders * padded_span),
    )
    answer_back = lax.all_to_all(
        answer.reshape(senders, query_share, head_share),
        "seq",
        split_axis=0,
        concat_axis=0,
        tiled=True,
    )
    attn_rows = (
        answer_back.reshape(requests, 2, halves, query_share, head_share)
        .transpose(2, 3, 0, 1, 4)
        .reshape(rows_all, features)
    )
    tp_index = lax.axis_index("tp")
    resident_mine = lax.dynamic_slice_in_dim(resident, tp_index * portion, portion, 0)
    attn_part = jnp.dot(attn_rows, w_out, preferred_element_type=jnp.float32).astype(jnp.bfloat16)
    attn_mixed = reduce_rows(attn_part, parties).reshape(portion, requests, model_width)
    after_attn = resident_mine + adaptive[:, 2] * attn_mixed
    mlp_mine = modulate(after_attn, adaptive[:, 3], adaptive[:, 4])
    mlp_in = lax.all_gather(mlp_mine, "tp", axis=0, tiled=True).reshape(rows_all, model_width)
    hidden = jax.nn.gelu(
        jnp.dot(mlp_in, w_up, preferred_element_type=jnp.float32), approximate=True
    ).astype(jnp.bfloat16)
    mlp_part = jnp.dot(hidden, w_down, preferred_element_type=jnp.float32).astype(jnp.bfloat16)
    mlp_grown = reduce_rows(mlp_part, parties).reshape(portion, requests, model_width)
    after_mlp = after_attn + adaptive[:, 5] * mlp_grown
    head_in = modulate(after_mlp, adaptive[:, 8], adaptive[:, 9]).reshape(
        portion * requests, model_width
    )
    velocity_own = jnp.dot(head_in, w_final, preferred_element_type=jnp.float32).reshape(
        portion, requests, w_final.shape[1]
    )
    half_width = w_final.shape[1] // 2
    cfg_index = lax.axis_index("cfg")
    own_kept = lax.dynamic_slice_in_dim(velocity_own, cfg_index * half_width, half_width, 2)
    own_given = lax.dynamic_slice_in_dim(velocity_own, (1 - cfg_index) * half_width, half_width, 2)
    velocity_other = swapped(own_given, "cfg", 0)
    is_first = cfg_index == 0
    guided_cond = jnp.where(is_first, own_kept, velocity_other)
    guided_free = jnp.where(is_first, velocity_other, own_kept)
    velocity = guided_free + GUIDANCE * (guided_cond - guided_free)
    steps_all = jnp.arange(sigmas.shape[0], dtype=jnp.int32)
    sigma_now = jnp.sum(
        jnp.where(steps_all[None, :] == timestep_index[:, None], sigmas[None, :], 0.0), 1
    )
    sigma_after = jnp.sum(
        jnp.where(steps_all[None, :] == timestep_index[:, None] + 1, sigmas[None, :], 0.0), 1
    )
    latent_next = latents + (sigma_after - sigma_now)[None, :, None] * velocity
    return (velocity, latent_next)


def solution(mesh):
    return jax.shard_map(
        shards,
        mesh=mesh,
        in_specs=(
            P("cfg", "seq", None, None),
            P("cfg", "seq", None, None),
            P("cfg", None, None, None),
            P("cfg", None),
            P(),
            P(),
            P(("seq", "tp"), None, "cfg"),
            P(None, None, "tp"),
            P(None, None, "tp"),
            P("tp", None),
            P(None, "tp"),
            P("tp", None),
            P(),
        ),
        out_specs=(P(("seq", "tp"), None, "cfg"), P(("seq", "tp"), None, "cfg")),
        check_vma=False,
    )
```

```python
import math

import jax
import jax.numpy as jnp
from jax import lax
from jax.experimental import pallas as pl
from jax.experimental.pallas import tpu as pltpu
from jax.sharding import PartitionSpec as P

HEAD_DIM = 64


EPSILON = 1e-06
GUIDANCE = 7.0


def swapped(value, axis, apart):
    return lax.ppermute(value, axis, [(i, i ^ 1 << apart) for i in range(lax.axis_size(axis))])


def layer_norm(values):
    center = values - jnp.mean(values, -1, keepdims=True)
    return center * lax.rsqrt(jnp.mean(center * center, -1, keepdims=True) + EPSILON)


def modulate(values, shift_add, scale_mul):
    return (layer_norm(values) * (1.0 + scale_mul) + shift_add).astype(jnp.bfloat16)


def attention_body(q_ref, k_ref, v_ref, valid_ref, o_ref):
    queries = q_ref[...]
    keys = k_ref[...]
    values = v_ref[...]
    valid = valid_ref[...] > 0.5
    width = queries.shape[1]
    lane_head = lax.broadcasted_iota(jnp.int32, (1, width), 1) // HEAD_DIM
    result = jnp.zeros(o_ref.shape, jnp.float32)
    for head in range(width // HEAD_DIM):
        chosen = lane_head == head
        query_head = jnp.where(chosen, queries, jnp.zeros_like(queries))
        scores = lax.dot_general(
            query_head, keys, (((1,), (1,)), ((), ())), preferred_element_type=jnp.float32
        ) * (1.0 / math.sqrt(HEAD_DIM))
        scores = jnp.where(valid, scores, -jnp.inf)
        row_max = jnp.max(scores, axis=1, keepdims=True)
        exp_scores = jnp.exp(scores - row_max)
        total = jnp.sum(exp_scores, axis=1, keepdims=True)
        weights = (exp_scores / total).astype(jnp.bfloat16)
        mixed = jnp.dot(weights, values, preferred_element_type=jnp.float32)
        result = jnp.where(chosen, mixed, result)
    o_ref[...] = result.astype(o_ref.dtype)


def attention_kernel(order_ref, q_ref, mine_ref, other_ref, valid_ref, o_ref):
    keys_first = order_ref[0] == 0

    @pl.when(keys_first)
    def _():
        attention_body(q_ref, mine_ref, other_ref, valid_ref, o_ref)

    @pl.when(jnp.logical_not(keys_first))
    def _():
        attention_body(q_ref, other_ref, mine_ref, valid_ref, o_ref)


def attend_kernel(order, queries, kv_mine, kv_other, valid):
    whole = pl.BlockSpec(memory_space=pltpu.VMEM)
    return pl.pallas_call(
        attention_kernel,
        out_shape=jax.ShapeDtypeStruct(queries.shape, jnp.bfloat16),
        in_specs=[pl.BlockSpec(memory_space=pltpu.SMEM), whole, whole, whole, whole],
        out_specs=whole,
    )(order, queries, kv_mine, kv_other, valid)


def reduce_rows(partial, parties):
    pieces = partial.reshape(parties, partial.shape[0] // parties, partial.shape[1])
    got = lax.all_to_all(pieces, "tp", split_axis=0, concat_axis=0, tiled=True)
    return jnp.sum(got.astype(jnp.float32), 0)


def shards(
    img_hidden,
    txt_hidden,
    modulation,
    text_lengths,
    timestep_index,
    sigmas,
    latents,
    w_qkv,
    w_kv_text,
    w_out,
    w_up,
    w_down,
    w_final,
):
    img_slice = img_hidden.shape[1]
    requests = img_hidden.shape[2]
    model_width = img_hidden.shape[3]
    txt_slice = txt_hidden.shape[1]
    features = w_out.shape[0]
    members = lax.axis_size("seq") // requests
    parties = lax.axis_size("tp")
    portion = img_slice // parties
    rows_all = img_slice * requests
    adaptive = modulation[0].astype(jnp.float32)
    resident = img_hidden[0].astype(jnp.float32)
    lengths_all = text_lengths[0]
    normed = modulate(resident, adaptive[:, 0], adaptive[:, 1]).reshape(rows_all, model_width)
    queries, keys_img, vals_img = [
        jnp.dot(normed, w_qkv[:, part], preferred_element_type=jnp.float32)
        .astype(jnp.bfloat16)
        .reshape(img_slice, requests, features)
        for part in range(3)
    ]
    text_in = modulate(txt_hidden[0].astype(jnp.float32), adaptive[:, 6], adaptive[:, 7]).reshape(
        txt_slice * requests, model_width
    )
    keys_txt, vals_txt = [
        jnp.dot(text_in, w_kv_text[:, part], preferred_element_type=jnp.float32)
        .astype(jnp.bfloat16)
        .reshape(txt_slice, requests, features)
        for part in range(2)
    ]
    key_span = img_slice + txt_slice
    senders = requests * members
    halves = members // 2
    query_share = img_slice // halves
    head_share = features // 2
    query_send = (
        queries.reshape(halves, query_share, requests, 2, head_share)
        .transpose(2, 3, 0, 1, 4)
        .reshape(senders, query_share, head_share)
    )
    joined_k = jnp.concatenate([keys_img, keys_txt], 0).reshape(key_span, requests, 2, head_share)
    joined_v = jnp.concatenate([vals_img, vals_txt], 0).reshape(key_span, requests, 2, head_share)
    kv_send = (
        jnp.stack([joined_k, joined_v], 3)
        .transpose(1, 2, 3, 0, 4)
        .reshape(senders, key_span, head_share)
    )
    payload = jnp.concatenate([query_send, kv_send], 1)
    got = lax.all_to_all(payload, "seq", split_axis=0, concat_axis=0, tiled=True)
    query_got = got[:, :query_share]
    kv_mine = got[:, query_share:]
    kv_other = swapped(kv_mine, "seq", 0)
    my_request = lax.axis_index("seq") // members
    length_now = jnp.sum(jnp.where(jnp.arange(requests) == my_request, lengths_all, 0))
    padded_span = -(-key_span // 8) * 8
    slot = jnp.arange(padded_span)
    text_slot = jnp.arange(senders)[:, None] * txt_slice + slot[None, :] - img_slice
    key_valid = (slot[None, :] < img_slice) | ((slot[None, :] < key_span) & (text_slot < length_now))

    def padded(block):
        return jnp.pad(block, ((0, 0), (0, padded_span - key_span), (0, 0))).reshape(
            senders * padded_span, head_share
        )

    answer = attend_kernel(
        (lax.axis_index("seq") % 2).reshape(1).astype(jnp.int32),
        query_got.reshape(senders * query_share, head_share),
        padded(kv_mine),
        padded(kv_other),
        key_valid.astype(jnp.float32).reshape(1, senders * padded_span),
    )
    answer_back = lax.all_to_all(
        answer.reshape(senders, query_share, head_share),
        "seq",
        split_axis=0,
        concat_axis=0,
        tiled=True,
    )
    attn_rows = (
        answer_back.reshape(requests, 2, halves, query_share, head_share)
        .transpose(2, 3, 0, 1, 4)
        .reshape(rows_all, features)
    )
    tp_index = lax.axis_index("tp")
    resident_mine = lax.dynamic_slice_in_dim(resident, tp_index * portion, portion, 0)
    attn_part = jnp.dot(attn_rows, w_out, preferred_element_type=jnp.float32).astype(jnp.bfloat16)
    attn_mixed = reduce_rows(attn_part, parties).reshape(portion, requests, model_width)
    after_attn = resident_mine + adaptive[:, 2] * attn_mixed
    mlp_mine = modulate(after_attn, adaptive[:, 3], adaptive[:, 4])
    mlp_in = lax.all_gather(mlp_mine, "tp", axis=0, tiled=True).reshape(rows_all, model_width)
    hidden = jax.nn.gelu(
        jnp.dot(mlp_in, w_up, preferred_element_type=jnp.float32), approximate=True
    ).astype(jnp.bfloat16)
    mlp_part = jnp.dot(hidden, w_down, preferred_element_type=jnp.float32).astype(jnp.bfloat16)
    mlp_grown = reduce_rows(mlp_part, parties).reshape(portion, requests, model_width)
    after_mlp = after_attn + adaptive[:, 5] * mlp_grown
    head_in = modulate(after_mlp, adaptive[:, 8], adaptive[:, 9]).reshape(
        portion * requests, model_width
    )
    velocity_own = jnp.dot(head_in, w_final, preferred_element_type=jnp.float32).reshape(
        portion, requests, w_final.shape[1]
    )
    half_width = w_final.shape[1] // 2
    cfg_index = lax.axis_index("cfg")
    own_kept = lax.dynamic_slice_in_dim(velocity_own, cfg_index * half_width, half_width, 2)
    own_given = lax.dynamic_slice_in_dim(velocity_own, (1 - cfg_index) * half_width, half_width, 2)
    velocity_other = swapped(own_given, "cfg", 0)
    is_first = cfg_index == 0
    guided_cond = jnp.where(is_first, own_kept, velocity_other)
    guided_free = jnp.where(is_first, velocity_other, own_kept)
    velocity = guided_free + GUIDANCE * (guided_cond - guided_free)
    steps_all = jnp.arange(sigmas.shape[0], dtype=jnp.int32)
    sigma_now = jnp.sum(
        jnp.where(steps_all[None, :] == timestep_index[:, None], sigmas[None, :], 0.0), 1
    )
    sigma_after = jnp.sum(
        jnp.where(steps_all[None, :] == timestep_index[:, None] + 1, sigmas[None, :], 0.0), 1
    )
    latent_next = latents + (sigma_after - sigma_now)[None, :, None] * velocity
    return (velocity, latent_next)


def solution(mesh):
    return jax.shard_map(
        shards,
        mesh=mesh,
        in_specs=(
            P("cfg", "seq", None, None),
            P("cfg", "seq", None, None),
            P("cfg", None, None, None),
            P("cfg", None),
            P(),
            P(),
            P(("seq", "tp"), None, "cfg"),
            P(None, None, "tp"),
            P(None, None, "tp"),
            P("tp", None),
            P(None, "tp"),
            P("tp", None),
            P(),
        ),
        out_specs=(P(("seq", "tp"), None, "cfg"), P(("seq", "tp"), None, "cfg")),
        check_vma=False,
    )
```

```python
import math

import jax
import jax.numpy as jnp
from jax import lax
from jax.experimental import pallas as pl
from jax.sharding import PartitionSpec as P

HEAD_DIM = 64


EPSILON = 1e-06
GUIDANCE = 7.0


def swapped(value, axis, apart):
    return lax.ppermute(value, axis, [(i, i ^ 1 << apart) for i in range(lax.axis_size(axis))])


def layer_norm(values):
    center = values - jnp.mean(values, -1, keepdims=True)
    return center * lax.rsqrt(jnp.mean(center * center, -1, keepdims=True) + EPSILON)


def modulate(values, shift_add, scale_mul):
    return (layer_norm(values) * (1.0 + scale_mul) + shift_add).astype(jnp.bfloat16)


def attention_kernel(q_ref, ki_ref, vi_ref, kt_ref, vt_ref, valid_ref, o_ref):
    queries = q_ref[...]
    keys_img = ki_ref[...]
    values_img = vi_ref[...]
    keys_txt = kt_ref[...]
    values_txt = vt_ref[...]
    valid = valid_ref[...] > 0.5
    width = queries.shape[1]
    lane_head = lax.broadcasted_iota(jnp.int32, (1, width), 1) // HEAD_DIM
    contract = (((1,), (1,)), ((), ()))
    scale = 1.0 / math.sqrt(HEAD_DIM)
    result = jnp.zeros(o_ref.shape, jnp.float32)
    for head in range(width // HEAD_DIM):
        chosen = lane_head == head
        query_head = jnp.where(chosen, queries, jnp.zeros_like(queries))
        scores_img = (
            lax.dot_general(query_head, keys_img, contract, preferred_element_type=jnp.float32)
            * scale
        )
        scores_txt = (
            lax.dot_general(query_head, keys_txt, contract, preferred_element_type=jnp.float32)
            * scale
        )
        scores_txt = jnp.where(valid, scores_txt, -jnp.inf)
        row_max = jnp.maximum(
            jnp.max(scores_img, axis=1, keepdims=True), jnp.max(scores_txt, axis=1, keepdims=True)
        )
        exp_img = jnp.exp(scores_img - row_max)
        exp_txt = jnp.exp(scores_txt - row_max)
        total = jnp.sum(exp_img, axis=1, keepdims=True) + jnp.sum(exp_txt, axis=1, keepdims=True)
        weights_img = (exp_img / total).astype(jnp.bfloat16)
        weights_txt = (exp_txt / total).astype(jnp.bfloat16)
        mixed = jnp.dot(weights_img, values_img, preferred_element_type=jnp.float32) + jnp.dot(
            weights_txt, values_txt, preferred_element_type=jnp.float32
        )
        result = jnp.where(chosen, mixed, result)
    o_ref[...] = result.astype(o_ref.dtype)


def attend_kernel(queries, keys_img, values_img, keys_txt, values_txt, valid):
    return pl.pallas_call(
        attention_kernel,
        out_shape=jax.ShapeDtypeStruct(queries.shape, jnp.bfloat16),
    )(queries, keys_img, values_img, keys_txt, values_txt, valid)


def reduce_rows(partial, parties):
    pieces = partial.reshape(parties, partial.shape[0] // parties, partial.shape[1])
    got = lax.all_to_all(pieces, "tp", split_axis=0, concat_axis=0, tiled=True)
    return jnp.sum(got.astype(jnp.float32), 0)


def shards(
    img_hidden,
    txt_hidden,
    modulation,
    text_lengths,
    timestep_index,
    sigmas,
    latents,
    w_qkv,
    w_kv_text,
    w_out,
    w_up,
    w_down,
    w_final,
):
    img_slice = img_hidden.shape[1]
    requests = img_hidden.shape[2]
    model_width = img_hidden.shape[3]
    txt_slice = txt_hidden.shape[1]
    features = w_out.shape[0]
    members = lax.axis_size("seq") // requests
    parties = lax.axis_size("tp")
    portion = img_slice // parties
    rows_all = img_slice * requests
    adaptive = modulation[0].astype(jnp.float32)
    resident = img_hidden[0].astype(jnp.float32)
    lengths_all = text_lengths[0]
    normed = modulate(resident, adaptive[:, 0], adaptive[:, 1]).reshape(rows_all, model_width)
    queries, keys_img, vals_img = [
        jnp.dot(normed, w_qkv[:, part], preferred_element_type=jnp.float32)
        .astype(jnp.bfloat16)
        .reshape(img_slice, requests, features)
        for part in range(3)
    ]
    text_in = modulate(txt_hidden[0].astype(jnp.float32), adaptive[:, 6], adaptive[:, 7]).reshape(
        txt_slice * requests, model_width
    )
    text_kv = jnp.dot(
        text_in, w_kv_text.reshape(model_width, 2 * features), preferred_element_type=jnp.float32
    ).astype(jnp.bfloat16)
    keys_txt = text_kv[:, :features].reshape(txt_slice, requests, features)
    vals_txt = text_kv[:, features:].reshape(txt_slice, requests, features)
    key_span = img_slice + txt_slice
    senders = requests * members
    halves = members // 2
    query_share = img_slice // halves
    head_share = features // 2
    query_send = (
        queries.reshape(halves, query_share, requests, 2, head_share)
        .transpose(2, 3, 0, 1, 4)
        .reshape(senders, query_share, head_share)
    )
    joined_k = jnp.concatenate([keys_img, keys_txt], 0).reshape(key_span, requests, 2, head_share)
    joined_v = jnp.concatenate([vals_img, vals_txt], 0).reshape(key_span, requests, 2, head_share)
    kv_send = (
        jnp.stack([joined_k, joined_v], 3)
        .transpose(1, 2, 3, 0, 4)
        .reshape(senders, key_span, head_share)
    )
    payload = jnp.concatenate([query_send, kv_send], 1)
    got = lax.all_to_all(payload, "seq", split_axis=0, concat_axis=0, tiled=True)
    query_got = got[:, :query_share]
    kv_mine = got[:, query_share:]
    kv_other = swapped(kv_mine, "seq", 0)
    first_core = lax.axis_index("seq") % 2 == 0
    key_got = jnp.where(first_core, kv_mine, kv_other)
    value_got = jnp.where(first_core, kv_other, kv_mine)
    my_request = lax.axis_index("seq") // members
    length_now = jnp.sum(jnp.where(jnp.arange(requests) == my_request, lengths_all, 0))
    text_rows = senders * txt_slice
    text_span = -(-text_rows // 128) * 128
    text_valid = jnp.arange(text_span) < jnp.minimum(length_now, text_rows)

    def image_part(block):
        return block[:, :img_slice].reshape(senders * img_slice, head_share)

    def text_part(block):
        return jnp.pad(
            block[:, img_slice:].reshape(text_rows, head_share), ((0, text_span - text_rows), (0, 0))
        )

    answer = attend_kernel(
        query_got.reshape(senders * query_share, head_share),
        image_part(key_got),
        image_part(value_got),
        text_part(key_got),
        text_part(value_got),
        text_valid.astype(jnp.float32).reshape(1, text_span),
    )
    answer_back = lax.all_to_all(
        answer.reshape(senders, query_share, head_share),
        "seq",
        split_axis=0,
        concat_axis=0,
        tiled=True,
    )
    attn_rows = (
        answer_back.reshape(requests, 2, halves, query_share, head_share)
        .transpose(2, 3, 0, 1, 4)
        .reshape(rows_all, features)
    )
    tp_index = lax.axis_index("tp")
    resident_mine = lax.dynamic_slice_in_dim(resident, tp_index * portion, portion, 0)
    attn_part = jnp.dot(attn_rows, w_out, preferred_element_type=jnp.float32).astype(jnp.bfloat16)
    attn_mixed = reduce_rows(attn_part, parties).reshape(portion, requests, model_width)
    after_attn = resident_mine + adaptive[:, 2] * attn_mixed
    mlp_mine = modulate(after_attn, adaptive[:, 3], adaptive[:, 4])
    mlp_in = lax.all_gather(mlp_mine, "tp", axis=0, tiled=True).reshape(rows_all, model_width)
    hidden = jax.nn.gelu(
        jnp.dot(mlp_in, w_up, preferred_element_type=jnp.float32), approximate=True
    ).astype(jnp.bfloat16)
    mlp_part = jnp.dot(hidden, w_down, preferred_element_type=jnp.float32).astype(jnp.bfloat16)
    mlp_grown = reduce_rows(mlp_part, parties).reshape(portion, requests, model_width)
    after_mlp = after_attn + adaptive[:, 5] * mlp_grown
    head_in = modulate(after_mlp, adaptive[:, 8], adaptive[:, 9]).reshape(
        portion * requests, model_width
    )
    velocity_own = jnp.dot(head_in, w_final, preferred_element_type=jnp.float32).reshape(
        portion, requests, w_final.shape[1]
    )
    half_width = w_final.shape[1] // 2
    cfg_index = lax.axis_index("cfg")
    own_kept = lax.dynamic_slice_in_dim(velocity_own, cfg_index * half_width, half_width, 2)
    own_given = lax.dynamic_slice_in_dim(velocity_own, (1 - cfg_index) * half_width, half_width, 2)
    velocity_other = swapped(own_given, "cfg", 0)
    is_first = cfg_index == 0
    guided_cond = jnp.where(is_first, own_kept, velocity_other)
    guided_free = jnp.where(is_first, velocity_other, own_kept)
    velocity = guided_free + GUIDANCE * (guided_cond - guided_free)
    steps_all = jnp.arange(sigmas.shape[0], dtype=jnp.int32)
    sigma_now = jnp.sum(
        jnp.where(steps_all[None, :] == timestep_index[:, None], sigmas[None, :], 0.0), 1
    )
    sigma_after = jnp.sum(
        jnp.where(steps_all[None, :] == timestep_index[:, None] + 1, sigmas[None, :], 0.0), 1
    )
    latent_next = latents + (sigma_after - sigma_now)[None, :, None] * velocity
    return (velocity, latent_next)


def solution(mesh):
    return jax.shard_map(
        shards,
        mesh=mesh,
        in_specs=(
            P("cfg", "seq", None, None),
            P("cfg", "seq", None, None),
            P("cfg", None, None, None),
            P("cfg", None),
            P(),
            P(),
            P(("seq", "tp"), None, "cfg"),
            P(None, None, "tp"),
            P(None, None, "tp"),
            P("tp", None),
            P(None, "tp"),
            P("tp", None),
            P(),
        ),
        out_specs=(P(("seq", "tp"), None, "cfg"), P(("seq", "tp"), None, "cfg")),
        check_vma=False,
    )
```

```python
import math

import jax
import jax.numpy as jnp
from jax import lax
from jax.experimental import pallas as pl
from jax.sharding import PartitionSpec as P

HEAD_DIM = 64


EPSILON = 1e-06
GUIDANCE = 7.0


def swapped(value, axis, apart):
    return lax.ppermute(value, axis, [(i, i ^ 1 << apart) for i in range(lax.axis_size(axis))])


def layer_norm(values):
    center = values - jnp.mean(values, -1, keepdims=True)
    return center * lax.rsqrt(jnp.mean(center * center, -1, keepdims=True) + EPSILON)


def modulate(values, shift_add, scale_mul):
    return (layer_norm(values) * (1.0 + scale_mul) + shift_add).astype(jnp.bfloat16)


def attention_kernel(q_ref, ki_ref, vi_ref, kt_ref, vt_ref, valid_ref, o_ref):
    queries = q_ref[...]
    keys_img = ki_ref[...]
    values_img = vi_ref[...]
    keys_txt = kt_ref[...]
    values_txt = vt_ref[...]
    valid = valid_ref[...] > 0.5
    width = queries.shape[1]
    lane_head = lax.broadcasted_iota(jnp.int32, (1, width), 1) // HEAD_DIM
    contract = (((1,), (1,)), ((), ()))
    scale = 1.0 / math.sqrt(HEAD_DIM)
    result = jnp.zeros(o_ref.shape, jnp.float32)
    for head in range(width // HEAD_DIM):
        chosen = lane_head == head
        query_head = jnp.where(chosen, queries, jnp.zeros_like(queries))
        scores_img = (
            lax.dot_general(query_head, keys_img, contract, preferred_element_type=jnp.float32)
            * scale
        )
        scores_txt = (
            lax.dot_general(query_head, keys_txt, contract, preferred_element_type=jnp.float32)
            * scale
        )
        scores_txt = jnp.where(valid, scores_txt, -jnp.inf)
        row_max = jnp.maximum(
            jnp.max(scores_img, axis=1, keepdims=True), jnp.max(scores_txt, axis=1, keepdims=True)
        )
        exp_img = jnp.exp(scores_img - row_max)
        exp_txt = jnp.exp(scores_txt - row_max)
        total = jnp.sum(exp_img, axis=1, keepdims=True) + jnp.sum(exp_txt, axis=1, keepdims=True)
        weights_img = (exp_img / total).astype(jnp.bfloat16)
        weights_txt = (exp_txt / total).astype(jnp.bfloat16)
        mixed = jnp.dot(weights_img, values_img, preferred_element_type=jnp.float32) + jnp.dot(
            weights_txt, values_txt, preferred_element_type=jnp.float32
        )
        result = jnp.where(chosen, mixed, result)
    o_ref[...] = result.astype(o_ref.dtype)


def attend_kernel(queries, keys_img, values_img, keys_txt, values_txt, valid):
    return pl.pallas_call(
        attention_kernel,
        out_shape=jax.ShapeDtypeStruct(queries.shape, jnp.bfloat16),
    )(queries, keys_img, values_img, keys_txt, values_txt, valid)


def reduce_rows(partial, parties):
    pieces = partial.reshape(parties, partial.shape[0] // parties, partial.shape[1])
    got = lax.all_to_all(pieces, "tp", split_axis=0, concat_axis=0, tiled=True)
    return jnp.sum(got.astype(jnp.float32), 0)


def shards(
    img_hidden,
    txt_hidden,
    modulation,
    text_lengths,
    timestep_index,
    sigmas,
    latents,
    w_qkv,
    w_kv_text,
    w_out,
    w_up,
    w_down,
    w_final,
):
    img_slice = img_hidden.shape[1]
    requests = img_hidden.shape[2]
    model_width = img_hidden.shape[3]
    txt_slice = txt_hidden.shape[1]
    features = w_out.shape[0]
    members = lax.axis_size("seq") // requests
    parties = lax.axis_size("tp")
    portion = img_slice // parties
    rows_all = img_slice * requests
    adaptive = modulation[0].astype(jnp.float32)
    resident = img_hidden[0].astype(jnp.float32)
    lengths_all = text_lengths[0]
    normed = modulate(resident, adaptive[:, 0], adaptive[:, 1]).reshape(rows_all, model_width)
    queries, keys_img, vals_img = [
        jnp.dot(normed, w_qkv[:, part], preferred_element_type=jnp.float32)
        .astype(jnp.bfloat16)
        .reshape(img_slice, requests, features)
        for part in range(3)
    ]
    text_in = modulate(txt_hidden[0].astype(jnp.float32), adaptive[:, 6], adaptive[:, 7]).reshape(
        txt_slice * requests, model_width
    )
    text_kv = jnp.dot(
        text_in, w_kv_text.reshape(model_width, 2 * features), preferred_element_type=jnp.float32
    ).astype(jnp.bfloat16)
    keys_txt = text_kv[:, :features].reshape(txt_slice, requests, features)
    vals_txt = text_kv[:, features:].reshape(txt_slice, requests, features)
    key_span = img_slice + txt_slice
    senders = requests * members
    halves = members // 2
    query_share = img_slice // halves
    head_share = features // 2
    query_send = (
        queries.reshape(halves, query_share, requests, 2, head_share)
        .transpose(2, 3, 0, 1, 4)
        .reshape(senders, query_share, head_share)
    )
    joined_k = jnp.concatenate([keys_img, keys_txt], 0).reshape(key_span, requests, 2, head_share)
    joined_v = jnp.concatenate([vals_img, vals_txt], 0).reshape(key_span, requests, 2, head_share)
    kv_send = (
        jnp.stack([joined_k, joined_v], 3)
        .transpose(1, 2, 3, 0, 4)
        .reshape(senders, key_span, head_share)
    )
    rows_sent = query_share + key_span
    rows_padded = -(-rows_sent // 8) * 8
    payload = jnp.concatenate(
        [query_send, kv_send, jnp.zeros((senders, rows_padded - rows_sent, head_share), kv_send.dtype)],
        1,
    )
    dense = payload.reshape(senders, rows_padded * head_share // 128, 128)
    got = lax.all_to_all(dense, "seq", split_axis=0, concat_axis=0, tiled=True).reshape(
        senders, rows_padded, head_share
    )[:, :rows_sent]
    query_got = got[:, :query_share]
    kv_mine = got[:, query_share:]
    kv_other = swapped(kv_mine, "seq", 0)
    first_core = lax.axis_index("seq") % 2 == 0
    key_got = jnp.where(first_core, kv_mine, kv_other)
    value_got = jnp.where(first_core, kv_other, kv_mine)
    my_request = lax.axis_index("seq") // members
    length_now = jnp.sum(jnp.where(jnp.arange(requests) == my_request, lengths_all, 0))
    text_rows = senders * txt_slice
    text_span = -(-text_rows // 128) * 128
    text_valid = jnp.arange(text_span) < jnp.minimum(length_now, text_rows)

    def image_part(block):
        return block[:, :img_slice].reshape(senders * img_slice, head_share)

    def text_part(block):
        return jnp.pad(
            block[:, img_slice:].reshape(text_rows, head_share), ((0, text_span - text_rows), (0, 0))
        )

    answer = attend_kernel(
        query_got.reshape(senders * query_share, head_share),
        image_part(key_got),
        image_part(value_got),
        text_part(key_got),
        text_part(value_got),
        text_valid.astype(jnp.float32).reshape(1, text_span),
    )
    answer_back = lax.all_to_all(
        answer.reshape(senders, query_share, head_share),
        "seq",
        split_axis=0,
        concat_axis=0,
        tiled=True,
    )
    attn_rows = (
        answer_back.reshape(requests, 2, halves, query_share, head_share)
        .transpose(2, 3, 0, 1, 4)
        .reshape(rows_all, features)
    )
    tp_index = lax.axis_index("tp")
    resident_mine = lax.dynamic_slice_in_dim(resident, tp_index * portion, portion, 0)
    attn_part = jnp.dot(attn_rows, w_out, preferred_element_type=jnp.float32).astype(jnp.bfloat16)
    attn_mixed = reduce_rows(attn_part, parties).reshape(portion, requests, model_width)
    after_attn = resident_mine + adaptive[:, 2] * attn_mixed
    mlp_mine = modulate(after_attn, adaptive[:, 3], adaptive[:, 4])
    mlp_in = lax.all_gather(mlp_mine, "tp", axis=0, tiled=True).reshape(rows_all, model_width)
    hidden = jax.nn.gelu(
        jnp.dot(mlp_in, w_up, preferred_element_type=jnp.float32), approximate=True
    ).astype(jnp.bfloat16)
    mlp_part = jnp.dot(hidden, w_down, preferred_element_type=jnp.float32).astype(jnp.bfloat16)
    mlp_grown = reduce_rows(mlp_part, parties).reshape(portion, requests, model_width)
    after_mlp = after_attn + adaptive[:, 5] * mlp_grown
    head_in = modulate(after_mlp, adaptive[:, 8], adaptive[:, 9]).reshape(
        portion * requests, model_width
    )
    velocity_own = jnp.dot(head_in, w_final, preferred_element_type=jnp.float32).reshape(
        portion, requests, w_final.shape[1]
    )
    half_width = w_final.shape[1] // 2
    cfg_index = lax.axis_index("cfg")
    own_kept = lax.dynamic_slice_in_dim(velocity_own, cfg_index * half_width, half_width, 2)
    own_given = lax.dynamic_slice_in_dim(velocity_own, (1 - cfg_index) * half_width, half_width, 2)
    velocity_other = swapped(own_given, "cfg", 0)
    is_first = cfg_index == 0
    guided_cond = jnp.where(is_first, own_kept, velocity_other)
    guided_free = jnp.where(is_first, velocity_other, own_kept)
    velocity = guided_free + GUIDANCE * (guided_cond - guided_free)
    steps_all = jnp.arange(sigmas.shape[0], dtype=jnp.int32)
    sigma_now = jnp.sum(
        jnp.where(steps_all[None, :] == timestep_index[:, None], sigmas[None, :], 0.0), 1
    )
    sigma_after = jnp.sum(
        jnp.where(steps_all[None, :] == timestep_index[:, None] + 1, sigmas[None, :], 0.0), 1
    )
    latent_next = latents + (sigma_after - sigma_now)[None, :, None] * velocity
    return (velocity, latent_next)


def solution(mesh):
    return jax.shard_map(
        shards,
        mesh=mesh,
        in_specs=(
            P("cfg", "seq", None, None),
            P("cfg", "seq", None, None),
            P("cfg", None, None, None),
            P("cfg", None),
            P(),
            P(),
            P(("seq", "tp"), None, "cfg"),
            P(None, None, "tp"),
            P(None, None, "tp"),
            P("tp", None),
            P(None, "tp"),
            P("tp", None),
            P(),
        ),
        out_specs=(P(("seq", "tp"), None, "cfg"), P(("seq", "tp"), None, "cfg")),
        check_vma=False,
    )
```

```python
import math

import jax
import jax.numpy as jnp
from jax import lax
from jax.experimental import pallas as pl
from jax.sharding import PartitionSpec as P

HEAD_DIM = 64


EPSILON = 1e-06
GUIDANCE = 7.0


def swapped(value, axis, apart):
    return lax.ppermute(value, axis, [(i, i ^ 1 << apart) for i in range(lax.axis_size(axis))])


def layer_norm(values):
    center = values - jnp.mean(values, -1, keepdims=True)
    return center * lax.rsqrt(jnp.mean(center * center, -1, keepdims=True) + EPSILON)


def modulate(values, shift_add, scale_mul):
    return (layer_norm(values) * (1.0 + scale_mul) + shift_add).astype(jnp.bfloat16)


def attention_kernel(q_ref, ki_ref, vi_ref, kt_ref, vt_ref, valid_ref, o_ref):
    queries = q_ref[...]
    keys_img = ki_ref[...]
    values_img = vi_ref[...]
    keys_txt = kt_ref[...]
    values_txt = vt_ref[...]
    valid = valid_ref[...] > 0.5
    width = queries.shape[1]
    lane_head = lax.broadcasted_iota(jnp.int32, (1, width), 1) // HEAD_DIM
    contract = (((1,), (1,)), ((), ()))
    scale = 1.0 / math.sqrt(HEAD_DIM)
    result = jnp.zeros(o_ref.shape, jnp.float32)
    for head in range(width // HEAD_DIM):
        chosen = lane_head == head
        query_head = jnp.where(chosen, queries, jnp.zeros_like(queries))
        scores_img = (
            lax.dot_general(query_head, keys_img, contract, preferred_element_type=jnp.float32)
            * scale
        )
        scores_txt = (
            lax.dot_general(query_head, keys_txt, contract, preferred_element_type=jnp.float32)
            * scale
        )
        scores_txt = jnp.where(valid, scores_txt, -jnp.inf)
        row_max = jnp.maximum(
            jnp.max(scores_img, axis=1, keepdims=True), jnp.max(scores_txt, axis=1, keepdims=True)
        )
        exp_img = jnp.exp(scores_img - row_max)
        exp_txt = jnp.exp(scores_txt - row_max)
        total = jnp.sum(exp_img, axis=1, keepdims=True) + jnp.sum(exp_txt, axis=1, keepdims=True)
        weights_img = (exp_img / total).astype(jnp.bfloat16)
        weights_txt = (exp_txt / total).astype(jnp.bfloat16)
        mixed = jnp.dot(weights_img, values_img, preferred_element_type=jnp.float32) + jnp.dot(
            weights_txt, values_txt, preferred_element_type=jnp.float32
        )
        result = jnp.where(chosen, mixed, result)
    o_ref[...] = result.astype(o_ref.dtype)


def attend_kernel(queries, keys_img, values_img, keys_txt, values_txt, valid):
    return pl.pallas_call(
        attention_kernel,
        out_shape=jax.ShapeDtypeStruct(queries.shape, jnp.bfloat16),
    )(queries, keys_img, values_img, keys_txt, values_txt, valid)


def shifted(value, axis, step):
    size = lax.axis_size(axis)
    return lax.ppermute(value, axis, [(i, (i + step) % size) for i in range(size)])


def reduce_rows(partial, parties):
    pieces = partial.reshape(parties, partial.shape[0] // parties, partial.shape[1])
    got = lax.all_to_all(pieces, "tp", split_axis=0, concat_axis=0, tiled=True)
    return jnp.sum(got.astype(jnp.float32), 0)


def shards(
    img_hidden,
    txt_hidden,
    modulation,
    text_lengths,
    timestep_index,
    sigmas,
    latents,
    w_qkv,
    w_kv_text,
    w_out,
    w_up,
    w_down,
    w_final,
):
    img_slice = img_hidden.shape[1]
    requests = img_hidden.shape[2]
    model_width = img_hidden.shape[3]
    txt_slice = txt_hidden.shape[1]
    features = w_out.shape[0]
    members = lax.axis_size("seq") // requests
    parties = lax.axis_size("tp")
    portion = img_slice // parties
    rows_all = img_slice * requests
    adaptive = modulation[0].astype(jnp.float32)
    resident = img_hidden[0].astype(jnp.float32)
    lengths_all = text_lengths[0]
    normed = modulate(resident, adaptive[:, 0], adaptive[:, 1]).reshape(rows_all, model_width)
    queries, keys_img, vals_img = [
        jnp.dot(normed, w_qkv[:, part], preferred_element_type=jnp.float32)
        .astype(jnp.bfloat16)
        .reshape(img_slice, requests, features)
        for part in range(3)
    ]
    text_in = modulate(txt_hidden[0].astype(jnp.float32), adaptive[:, 6], adaptive[:, 7]).reshape(
        txt_slice * requests, model_width
    )
    text_kv = jnp.dot(
        text_in, w_kv_text.reshape(model_width, 2 * features), preferred_element_type=jnp.float32
    ).astype(jnp.bfloat16)
    keys_txt = text_kv[:, :features].reshape(txt_slice, requests, features)
    vals_txt = text_kv[:, features:].reshape(txt_slice, requests, features)
    key_span = img_slice + txt_slice
    senders = requests * members
    halves = members // 2
    query_share = img_slice // halves
    head_share = features // 2
    query_send = (
        queries.reshape(halves, query_share, requests, 2, head_share)
        .transpose(2, 3, 0, 1, 4)
        .reshape(senders, query_share, head_share)
    )
    joined_k = jnp.concatenate([keys_img, keys_txt], 0).reshape(key_span, requests, 2, head_share)
    joined_v = jnp.concatenate([vals_img, vals_txt], 0).reshape(key_span, requests, 2, head_share)
    kv_send = (
        jnp.stack([joined_k, joined_v], 3)
        .transpose(1, 2, 3, 0, 4)
        .reshape(senders, key_span, head_share)
    )
    payload = jnp.concatenate([query_send, kv_send], 1)
    got = lax.all_to_all(payload, "seq", split_axis=0, concat_axis=0, tiled=True)
    query_got = got[:, :query_share]
    kv_mine = got[:, query_share:]
    kv_other = swapped(kv_mine, "seq", 0)
    first_core = lax.axis_index("seq") % 2 == 0
    key_got = jnp.where(first_core, kv_mine, kv_other)
    value_got = jnp.where(first_core, kv_other, kv_mine)
    my_request = lax.axis_index("seq") // members
    length_now = jnp.sum(jnp.where(jnp.arange(requests) == my_request, lengths_all, 0))
    text_rows = senders * txt_slice
    text_span = -(-text_rows // 128) * 128
    text_valid = jnp.arange(text_span) < jnp.minimum(length_now, text_rows)

    def image_part(block):
        return block[:, :img_slice].reshape(senders * img_slice, head_share)

    def text_part(block):
        return jnp.pad(
            block[:, img_slice:].reshape(text_rows, head_share), ((0, text_span - text_rows), (0, 0))
        )

    answer = attend_kernel(
        query_got.reshape(senders * query_share, head_share),
        image_part(key_got),
        image_part(value_got),
        text_part(key_got),
        text_part(value_got),
        text_valid.astype(jnp.float32).reshape(1, text_span),
    )
    answer_back = lax.all_to_all(
        answer.reshape(senders, query_share, head_share),
        "seq",
        split_axis=0,
        concat_axis=0,
        tiled=True,
    )
    attn_rows = (
        answer_back.reshape(requests, 2, halves, query_share, head_share)
        .transpose(2, 3, 0, 1, 4)
        .reshape(rows_all, features)
    )
    tp_index = lax.axis_index("tp")
    resident_mine = lax.dynamic_slice_in_dim(resident, tp_index * portion, portion, 0)
    attn_part = jnp.dot(attn_rows, w_out, preferred_element_type=jnp.float32).astype(jnp.bfloat16)
    attn_mixed = reduce_rows(attn_part, parties).reshape(portion, requests, model_width)
    after_attn = resident_mine + adaptive[:, 2] * attn_mixed
    mlp_mine = modulate(after_attn, adaptive[:, 3], adaptive[:, 4])
    arrived = [mlp_mine] + [shifted(mlp_mine, "tp", step) for step in range(1, parties)]
    mlp_total = None
    for step, block in enumerate(arrived):
        hidden = jax.nn.gelu(
            jnp.dot(
                block.reshape(portion * requests, model_width),
                w_up,
                preferred_element_type=jnp.float32,
            ),
            approximate=True,
        ).astype(jnp.bfloat16)
        part = jnp.dot(hidden, w_down, preferred_element_type=jnp.float32).astype(jnp.bfloat16)
        if step:
            part = shifted(part, "tp", -step)
        mlp_total = part.astype(jnp.float32) if mlp_total is None else mlp_total + part.astype(jnp.float32)
    mlp_grown = mlp_total.reshape(portion, requests, model_width)
    after_mlp = after_attn + adaptive[:, 5] * mlp_grown
    head_in = modulate(after_mlp, adaptive[:, 8], adaptive[:, 9]).reshape(
        portion * requests, model_width
    )
    velocity_own = jnp.dot(head_in, w_final, preferred_element_type=jnp.float32).reshape(
        portion, requests, w_final.shape[1]
    )
    half_width = w_final.shape[1] // 2
    cfg_index = lax.axis_index("cfg")
    own_kept = lax.dynamic_slice_in_dim(velocity_own, cfg_index * half_width, half_width, 2)
    own_given = lax.dynamic_slice_in_dim(velocity_own, (1 - cfg_index) * half_width, half_width, 2)
    velocity_other = swapped(own_given, "cfg", 0)
    is_first = cfg_index == 0
    guided_cond = jnp.where(is_first, own_kept, velocity_other)
    guided_free = jnp.where(is_first, velocity_other, own_kept)
    velocity = guided_free + GUIDANCE * (guided_cond - guided_free)
    steps_all = jnp.arange(sigmas.shape[0], dtype=jnp.int32)
    sigma_now = jnp.sum(
        jnp.where(steps_all[None, :] == timestep_index[:, None], sigmas[None, :], 0.0), 1
    )
    sigma_after = jnp.sum(
        jnp.where(steps_all[None, :] == timestep_index[:, None] + 1, sigmas[None, :], 0.0), 1
    )
    latent_next = latents + (sigma_after - sigma_now)[None, :, None] * velocity
    return (velocity, latent_next)


def solution(mesh):
    return jax.shard_map(
        shards,
        mesh=mesh,
        in_specs=(
            P("cfg", "seq", None, None),
            P("cfg", "seq", None, None),
            P("cfg", None, None, None),
            P("cfg", None),
            P(),
            P(),
            P(("seq", "tp"), None, "cfg"),
            P(None, None, "tp"),
            P(None, None, "tp"),
            P("tp", None),
            P(None, "tp"),
            P("tp", None),
            P(),
        ),
        out_specs=(P(("seq", "tp"), None, "cfg"), P(("seq", "tp"), None, "cfg")),
        check_vma=False,
    )
```

```python
import math

import jax
import jax.numpy as jnp
from jax import lax
from jax.experimental import pallas as pl
from jax.sharding import PartitionSpec as P

HEAD_DIM = 64


EPSILON = 1e-06
GUIDANCE = 7.0


def swapped(value, axis, apart):
    return lax.ppermute(value, axis, [(i, i ^ 1 << apart) for i in range(lax.axis_size(axis))])


def layer_norm(values):
    center = values - jnp.mean(values, -1, keepdims=True)
    return center * lax.rsqrt(jnp.mean(center * center, -1, keepdims=True) + EPSILON)


def modulate(values, shift_add, scale_mul):
    return (layer_norm(values) * (1.0 + scale_mul) + shift_add).astype(jnp.bfloat16)


def attention_kernel(q_ref, ki_ref, vi_ref, kt_ref, vt_ref, valid_ref, o_ref):
    queries = q_ref[...]
    keys_img = ki_ref[...]
    values_img = vi_ref[...]
    keys_txt = kt_ref[...]
    values_txt = vt_ref[...]
    valid = valid_ref[...] > 0.5
    width = queries.shape[1]
    lane_head = lax.broadcasted_iota(jnp.int32, (1, width), 1) // HEAD_DIM
    contract = (((1,), (1,)), ((), ()))
    scale = 1.0 / math.sqrt(HEAD_DIM)
    result = jnp.zeros(o_ref.shape, jnp.float32)
    for head in range(width // HEAD_DIM):
        chosen = lane_head == head
        query_head = jnp.where(chosen, queries, jnp.zeros_like(queries))
        scores_img = (
            lax.dot_general(query_head, keys_img, contract, preferred_element_type=jnp.float32)
            * scale
        )
        scores_txt = (
            lax.dot_general(query_head, keys_txt, contract, preferred_element_type=jnp.float32)
            * scale
        )
        scores_txt = jnp.where(valid, scores_txt, -jnp.inf)
        row_max = jnp.maximum(
            jnp.max(scores_img, axis=1, keepdims=True), jnp.max(scores_txt, axis=1, keepdims=True)
        )
        exp_img = jnp.exp(scores_img - row_max)
        exp_txt = jnp.exp(scores_txt - row_max)
        total = jnp.sum(exp_img, axis=1, keepdims=True) + jnp.sum(exp_txt, axis=1, keepdims=True)
        weights_img = (exp_img / total).astype(jnp.bfloat16)
        weights_txt = (exp_txt / total).astype(jnp.bfloat16)
        mixed = jnp.dot(weights_img, values_img, preferred_element_type=jnp.float32) + jnp.dot(
            weights_txt, values_txt, preferred_element_type=jnp.float32
        )
        result = jnp.where(chosen, mixed, result)
    o_ref[...] = result.astype(o_ref.dtype)


def attend_kernel(queries, keys_img, values_img, keys_txt, values_txt, valid):
    return pl.pallas_call(
        attention_kernel,
        out_shape=jax.ShapeDtypeStruct(queries.shape, jnp.bfloat16),
    )(queries, keys_img, values_img, keys_txt, values_txt, valid)


def shifted(value, axis, step):
    size = lax.axis_size(axis)
    return lax.ppermute(value, axis, [(i, (i + step) % size) for i in range(size)])


def shards(
    img_hidden,
    txt_hidden,
    modulation,
    text_lengths,
    timestep_index,
    sigmas,
    latents,
    w_qkv,
    w_kv_text,
    w_out,
    w_up,
    w_down,
    w_final,
):
    img_slice = img_hidden.shape[1]
    requests = img_hidden.shape[2]
    model_width = img_hidden.shape[3]
    txt_slice = txt_hidden.shape[1]
    features = w_out.shape[0]
    members = lax.axis_size("seq") // requests
    parties = lax.axis_size("tp")
    portion = img_slice // parties
    rows_all = img_slice * requests
    adaptive = modulation[0].astype(jnp.float32)
    resident = img_hidden[0].astype(jnp.float32)
    lengths_all = text_lengths[0]
    normed = modulate(resident, adaptive[:, 0], adaptive[:, 1]).reshape(rows_all, model_width)
    queries, keys_img, vals_img = [
        jnp.dot(normed, w_qkv[:, part], preferred_element_type=jnp.float32)
        .astype(jnp.bfloat16)
        .reshape(img_slice, requests, features)
        for part in range(3)
    ]
    text_in = modulate(txt_hidden[0].astype(jnp.float32), adaptive[:, 6], adaptive[:, 7]).reshape(
        txt_slice * requests, model_width
    )
    text_kv = jnp.dot(
        text_in, w_kv_text.reshape(model_width, 2 * features), preferred_element_type=jnp.float32
    ).astype(jnp.bfloat16)
    keys_txt = text_kv[:, :features].reshape(txt_slice, requests, features)
    vals_txt = text_kv[:, features:].reshape(txt_slice, requests, features)
    key_span = img_slice + txt_slice
    senders = requests * members
    halves = members // 2
    query_share = img_slice // halves
    head_share = features // 2
    query_send = (
        queries.reshape(halves, query_share, requests, 2, head_share)
        .transpose(2, 3, 0, 1, 4)
        .reshape(senders, query_share, head_share)
    )
    joined_k = jnp.concatenate([keys_img, keys_txt], 0).reshape(key_span, requests, 2, head_share)
    joined_v = jnp.concatenate([vals_img, vals_txt], 0).reshape(key_span, requests, 2, head_share)
    kv_send = (
        jnp.stack([joined_k, joined_v], 3)
        .transpose(1, 2, 3, 0, 4)
        .reshape(senders, key_span, head_share)
    )
    payload = jnp.concatenate([query_send, kv_send], 1)
    got = lax.all_to_all(payload, "seq", split_axis=0, concat_axis=0, tiled=True)
    query_got = got[:, :query_share]
    kv_mine = got[:, query_share:]
    kv_other = swapped(kv_mine, "seq", 0)
    first_core = lax.axis_index("seq") % 2 == 0
    key_got = jnp.where(first_core, kv_mine, kv_other)
    value_got = jnp.where(first_core, kv_other, kv_mine)
    my_request = lax.axis_index("seq") // members
    length_now = jnp.sum(jnp.where(jnp.arange(requests) == my_request, lengths_all, 0))
    text_rows = senders * txt_slice
    text_span = -(-text_rows // 128) * 128
    text_valid = jnp.arange(text_span) < jnp.minimum(length_now, text_rows)

    def image_part(block):
        return block[:, :img_slice].reshape(senders * img_slice, head_share)

    def text_part(block):
        return jnp.pad(
            block[:, img_slice:].reshape(text_rows, head_share), ((0, text_span - text_rows), (0, 0))
        )

    answer = attend_kernel(
        query_got.reshape(senders * query_share, head_share),
        image_part(key_got),
        image_part(value_got),
        text_part(key_got),
        text_part(value_got),
        text_valid.astype(jnp.float32).reshape(1, text_span),
    )
    answer_back = lax.all_to_all(
        answer.reshape(senders, query_share, head_share),
        "seq",
        split_axis=0,
        concat_axis=0,
        tiled=True,
    )
    attn_rows = (
        answer_back.reshape(requests, 2, halves, query_share, head_share)
        .transpose(2, 3, 0, 1, 4)
        .reshape(rows_all, features)
    )
    tp_index = lax.axis_index("tp")
    resident_mine = lax.dynamic_slice_in_dim(resident, tp_index * portion, portion, 0)
    block_rows = portion * requests
    attn_total = None
    for step in range(parties):
        rows_for = lax.dynamic_slice_in_dim(
            attn_rows, ((tp_index + step) % parties) * block_rows, block_rows, 0
        )
        part = jnp.dot(rows_for, w_out, preferred_element_type=jnp.float32).astype(jnp.bfloat16)
        if step:
            part = shifted(part, "tp", step)
        attn_total = (
            part.astype(jnp.float32) if attn_total is None else attn_total + part.astype(jnp.float32)
        )
    attn_mixed = attn_total.reshape(portion, requests, model_width)
    after_attn = resident_mine + adaptive[:, 2] * attn_mixed
    mlp_mine = modulate(after_attn, adaptive[:, 3], adaptive[:, 4])
    arrived = [mlp_mine] + [shifted(mlp_mine, "tp", step) for step in range(1, parties)]
    mlp_total = None
    for step, block in enumerate(arrived):
        hidden = jax.nn.gelu(
            jnp.dot(
                block.reshape(portion * requests, model_width),
                w_up,
                preferred_element_type=jnp.float32,
            ),
            approximate=True,
        ).astype(jnp.bfloat16)
        part = jnp.dot(hidden, w_down, preferred_element_type=jnp.float32).astype(jnp.bfloat16)
        if step:
            part = shifted(part, "tp", -step)
        mlp_total = part.astype(jnp.float32) if mlp_total is None else mlp_total + part.astype(jnp.float32)
    mlp_grown = mlp_total.reshape(portion, requests, model_width)
    after_mlp = after_attn + adaptive[:, 5] * mlp_grown
    head_in = modulate(after_mlp, adaptive[:, 8], adaptive[:, 9]).reshape(
        portion * requests, model_width
    )
    velocity_own = jnp.dot(head_in, w_final, preferred_element_type=jnp.float32).reshape(
        portion, requests, w_final.shape[1]
    )
    half_width = w_final.shape[1] // 2
    cfg_index = lax.axis_index("cfg")
    own_kept = lax.dynamic_slice_in_dim(velocity_own, cfg_index * half_width, half_width, 2)
    own_given = lax.dynamic_slice_in_dim(velocity_own, (1 - cfg_index) * half_width, half_width, 2)
    velocity_other = swapped(own_given, "cfg", 0)
    is_first = cfg_index == 0
    guided_cond = jnp.where(is_first, own_kept, velocity_other)
    guided_free = jnp.where(is_first, velocity_other, own_kept)
    velocity = guided_free + GUIDANCE * (guided_cond - guided_free)
    steps_all = jnp.arange(sigmas.shape[0], dtype=jnp.int32)
    sigma_now = jnp.sum(
        jnp.where(steps_all[None, :] == timestep_index[:, None], sigmas[None, :], 0.0), 1
    )
    sigma_after = jnp.sum(
        jnp.where(steps_all[None, :] == timestep_index[:, None] + 1, sigmas[None, :], 0.0), 1
    )
    latent_next = latents + (sigma_after - sigma_now)[None, :, None] * velocity
    return (velocity, latent_next)


def solution(mesh):
    return jax.shard_map(
        shards,
        mesh=mesh,
        in_specs=(
            P("cfg", "seq", None, None),
            P("cfg", "seq", None, None),
            P("cfg", None, None, None),
            P("cfg", None),
            P(),
            P(),
            P(("seq", "tp"), None, "cfg"),
            P(None, None, "tp"),
            P(None, None, "tp"),
            P("tp", None),
            P(None, "tp"),
            P("tp", None),
            P(),
        ),
        out_specs=(P(("seq", "tp"), None, "cfg"), P(("seq", "tp"), None, "cfg")),
        check_vma=False,
    )
```

```python
import math

import jax
import jax.numpy as jnp
from jax import lax
from jax.experimental import pallas as pl
from jax.sharding import PartitionSpec as P

HEAD_DIM = 64


EPSILON = 1e-06
GUIDANCE = 7.0


def swapped(value, axis, apart):
    return lax.ppermute(value, axis, [(i, i ^ 1 << apart) for i in range(lax.axis_size(axis))])


def layer_norm(values):
    center = values - jnp.mean(values, -1, keepdims=True)
    return center * lax.rsqrt(jnp.mean(center * center, -1, keepdims=True) + EPSILON)


def modulate(values, shift_add, scale_mul):
    return (layer_norm(values) * (1.0 + scale_mul) + shift_add).astype(jnp.bfloat16)


def attention_kernel(q_ref, ki_ref, vi_ref, kt_ref, vt_ref, valid_ref, o_ref):
    queries = q_ref[...]
    keys_img = ki_ref[...]
    values_img = vi_ref[...]
    keys_txt = kt_ref[...]
    values_txt = vt_ref[...]
    valid = valid_ref[...] > 0.5
    width = queries.shape[1]
    lane_head = lax.broadcasted_iota(jnp.int32, (1, width), 1) // HEAD_DIM
    contract = (((1,), (1,)), ((), ()))
    scale = 1.0 / math.sqrt(HEAD_DIM)
    result = jnp.zeros(o_ref.shape, jnp.float32)
    for head in range(width // HEAD_DIM):
        chosen = lane_head == head
        query_head = jnp.where(chosen, queries, jnp.zeros_like(queries))
        scores_img = (
            lax.dot_general(query_head, keys_img, contract, preferred_element_type=jnp.float32)
            * scale
        )
        scores_txt = (
            lax.dot_general(query_head, keys_txt, contract, preferred_element_type=jnp.float32)
            * scale
        )
        scores_txt = jnp.where(valid, scores_txt, -jnp.inf)
        row_max = jnp.maximum(
            jnp.max(scores_img, axis=1, keepdims=True), jnp.max(scores_txt, axis=1, keepdims=True)
        )
        exp_img = jnp.exp(scores_img - row_max)
        exp_txt = jnp.exp(scores_txt - row_max)
        total = jnp.sum(exp_img, axis=1, keepdims=True) + jnp.sum(exp_txt, axis=1, keepdims=True)
        weights_img = (exp_img / total).astype(jnp.bfloat16)
        weights_txt = (exp_txt / total).astype(jnp.bfloat16)
        mixed = jnp.dot(weights_img, values_img, preferred_element_type=jnp.float32) + jnp.dot(
            weights_txt, values_txt, preferred_element_type=jnp.float32
        )
        result = jnp.where(chosen, mixed, result)
    o_ref[...] = result.astype(o_ref.dtype)


def attend_kernel(queries, keys_img, values_img, keys_txt, values_txt, valid):
    return pl.pallas_call(
        attention_kernel,
        out_shape=jax.ShapeDtypeStruct(queries.shape, jnp.bfloat16),
    )(queries, keys_img, values_img, keys_txt, values_txt, valid)


def shifted(value, axis, step):
    size = lax.axis_size(axis)
    return lax.ppermute(value, axis, [(i, (i + step) % size) for i in range(size)])


def shards(
    img_hidden,
    txt_hidden,
    modulation,
    text_lengths,
    timestep_index,
    sigmas,
    latents,
    w_qkv,
    w_kv_text,
    w_out,
    w_up,
    w_down,
    w_final,
):
    img_slice = img_hidden.shape[1]
    requests = img_hidden.shape[2]
    model_width = img_hidden.shape[3]
    txt_slice = txt_hidden.shape[1]
    features = w_out.shape[0]
    members = lax.axis_size("seq") // requests
    parties = lax.axis_size("tp")
    portion = img_slice // parties
    rows_all = img_slice * requests
    adaptive = modulation[0].astype(jnp.float32)
    resident = img_hidden[0].astype(jnp.float32)
    lengths_all = text_lengths[0]
    normed = modulate(resident, adaptive[:, 0], adaptive[:, 1]).reshape(rows_all, model_width)
    queries, keys_img, vals_img = [
        jnp.dot(normed, w_qkv[:, part], preferred_element_type=jnp.float32)
        .astype(jnp.bfloat16)
        .reshape(img_slice, requests, features)
        for part in range(3)
    ]
    text_in = modulate(txt_hidden[0].astype(jnp.float32), adaptive[:, 6], adaptive[:, 7]).reshape(
        txt_slice * requests, model_width
    )
    text_kv = jnp.dot(
        text_in, w_kv_text.reshape(model_width, 2 * features), preferred_element_type=jnp.float32
    ).astype(jnp.bfloat16)
    keys_txt = text_kv[:, :features].reshape(txt_slice, requests, features)
    vals_txt = text_kv[:, features:].reshape(txt_slice, requests, features)
    key_span = img_slice + txt_slice
    senders = requests * members
    halves = members // 2
    query_share = img_slice // halves
    head_share = features // 2
    query_send = (
        queries.reshape(halves, query_share, requests, 2, head_share)
        .transpose(2, 3, 0, 1, 4)
        .reshape(senders, query_share, head_share)
    )
    joined_k = jnp.concatenate([keys_img, keys_txt], 0).reshape(key_span, requests, 2, head_share)
    joined_v = jnp.concatenate([vals_img, vals_txt], 0).reshape(key_span, requests, 2, head_share)
    kv_send = (
        jnp.stack([joined_k, joined_v], 3)
        .transpose(1, 2, 3, 0, 4)
        .reshape(senders, key_span, head_share)
    )
    payload = jnp.concatenate([query_send, kv_send], 1)
    got = lax.all_to_all(payload, "seq", split_axis=0, concat_axis=0, tiled=True)
    query_got = got[:, :query_share]
    kv_mine = got[:, query_share:]
    kv_other = swapped(kv_mine, "seq", 0)
    first_core = lax.axis_index("seq") % 2 == 0
    key_got = jnp.where(first_core, kv_mine, kv_other)
    value_got = jnp.where(first_core, kv_other, kv_mine)
    my_request = lax.axis_index("seq") // members
    length_now = jnp.sum(jnp.where(jnp.arange(requests) == my_request, lengths_all, 0))
    text_rows = senders * txt_slice
    text_span = -(-text_rows // 128) * 128
    text_valid = jnp.arange(text_span) < jnp.minimum(length_now, text_rows)

    def image_part(block):
        return block[:, :img_slice].reshape(senders * img_slice, head_share)

    def text_part(block):
        return jnp.pad(
            block[:, img_slice:].reshape(text_rows, head_share), ((0, text_span - text_rows), (0, 0))
        )

    answer = attend_kernel(
        query_got.reshape(senders * query_share, head_share),
        image_part(key_got),
        image_part(value_got),
        text_part(key_got),
        text_part(value_got),
        text_valid.astype(jnp.float32).reshape(1, text_span),
    )
    answer_back = lax.all_to_all(
        answer.reshape(senders, query_share, head_share),
        "seq",
        split_axis=0,
        concat_axis=0,
        tiled=True,
    )
    attn_rows = (
        answer_back.reshape(requests, 2, halves, query_share, head_share)
        .transpose(2, 3, 0, 1, 4)
        .reshape(rows_all, features)
    )
    tp_index = lax.axis_index("tp")
    resident_mine = lax.dynamic_slice_in_dim(img_hidden[0], tp_index * portion, portion, 0).astype(
        jnp.float32
    )
    block_rows = portion * requests
    attn_total = None
    for step in range(parties):
        rows_for = lax.dynamic_slice_in_dim(
            attn_rows, ((tp_index + step) % parties) * block_rows, block_rows, 0
        )
        part = jnp.dot(rows_for, w_out, preferred_element_type=jnp.float32).astype(jnp.bfloat16)
        if step:
            part = shifted(part, "tp", step)
        attn_total = (
            part.astype(jnp.float32) if attn_total is None else attn_total + part.astype(jnp.float32)
        )
    attn_mixed = attn_total.reshape(portion, requests, model_width)
    after_attn = resident_mine + adaptive[:, 2] * attn_mixed
    mlp_mine = modulate(after_attn, adaptive[:, 3], adaptive[:, 4])
    arrived = [mlp_mine] + [shifted(mlp_mine, "tp", step) for step in range(1, parties)]
    mlp_total = None
    for step, block in enumerate(arrived):
        hidden = jax.nn.gelu(
            jnp.dot(
                block.reshape(portion * requests, model_width),
                w_up,
                preferred_element_type=jnp.float32,
            ),
            approximate=True,
        ).astype(jnp.bfloat16)
        part = jnp.dot(hidden, w_down, preferred_element_type=jnp.float32).astype(jnp.bfloat16)
        if step:
            part = shifted(part, "tp", -step)
        mlp_total = part.astype(jnp.float32) if mlp_total is None else mlp_total + part.astype(jnp.float32)
    mlp_grown = mlp_total.reshape(portion, requests, model_width)
    after_mlp = after_attn + adaptive[:, 5] * mlp_grown
    head_in = modulate(after_mlp, adaptive[:, 8], adaptive[:, 9]).reshape(
        portion * requests, model_width
    )
    velocity_own = jnp.dot(head_in, w_final, preferred_element_type=jnp.float32).reshape(
        portion, requests, w_final.shape[1]
    )
    half_width = w_final.shape[1] // 2
    cfg_index = lax.axis_index("cfg")
    own_kept = lax.dynamic_slice_in_dim(velocity_own, cfg_index * half_width, half_width, 2)
    own_given = lax.dynamic_slice_in_dim(velocity_own, (1 - cfg_index) * half_width, half_width, 2)
    velocity_other = swapped(own_given, "cfg", 0)
    is_first = cfg_index == 0
    guided_cond = jnp.where(is_first, own_kept, velocity_other)
    guided_free = jnp.where(is_first, velocity_other, own_kept)
    velocity = guided_free + GUIDANCE * (guided_cond - guided_free)
    steps_all = jnp.arange(sigmas.shape[0], dtype=jnp.int32)
    sigma_now = jnp.sum(
        jnp.where(steps_all[None, :] == timestep_index[:, None], sigmas[None, :], 0.0), 1
    )
    sigma_after = jnp.sum(
        jnp.where(steps_all[None, :] == timestep_index[:, None] + 1, sigmas[None, :], 0.0), 1
    )
    latent_next = latents + (sigma_after - sigma_now)[None, :, None] * velocity
    return (velocity, latent_next)


def solution(mesh):
    return jax.shard_map(
        shards,
        mesh=mesh,
        in_specs=(
            P("cfg", "seq", None, None),
            P("cfg", "seq", None, None),
            P("cfg", None, None, None),
            P("cfg", None),
            P(),
            P(),
            P(("seq", "tp"), None, "cfg"),
            P(None, None, "tp"),
            P(None, None, "tp"),
            P("tp", None),
            P(None, "tp"),
            P("tp", None),
            P(),
        ),
        out_specs=(P(("seq", "tp"), None, "cfg"), P(("seq", "tp"), None, "cfg")),
        check_vma=False,
    )
```

```python
import math

import jax
import jax.numpy as jnp
from jax import lax
from jax.experimental import pallas as pl
from jax.sharding import PartitionSpec as P

HEAD_DIM = 64


EPSILON = 1e-06
GUIDANCE = 7.0


def swapped(value, axis, apart):
    return lax.ppermute(value, axis, [(i, i ^ 1 << apart) for i in range(lax.axis_size(axis))])


def layer_norm(values):
    center = values - jnp.mean(values, -1, keepdims=True)
    return center * lax.rsqrt(jnp.mean(center * center, -1, keepdims=True) + EPSILON)


def modulate(values, shift_add, scale_mul):
    return (layer_norm(values) * (1.0 + scale_mul) + shift_add).astype(jnp.bfloat16)


def attention_kernel(q_ref, ki_ref, vi_ref, kt_ref, vt_ref, valid_ref, o_ref):
    queries = q_ref[...]
    keys_img = ki_ref[...]
    values_img = vi_ref[...]
    keys_txt = kt_ref[...]
    values_txt = vt_ref[...]
    valid = valid_ref[...] > 0.5
    width = queries.shape[1]
    lane_head = lax.broadcasted_iota(jnp.int32, (1, width), 1) // HEAD_DIM
    contract = (((1,), (1,)), ((), ()))
    scale = 1.0 / math.sqrt(HEAD_DIM)
    result = jnp.zeros(o_ref.shape, jnp.float32)
    for head in range(width // HEAD_DIM):
        chosen = lane_head == head
        query_head = jnp.where(chosen, queries, jnp.zeros_like(queries))
        scores_img = (
            lax.dot_general(query_head, keys_img, contract, preferred_element_type=jnp.float32)
            * scale
        )
        scores_txt = (
            lax.dot_general(query_head, keys_txt, contract, preferred_element_type=jnp.float32)
            * scale
        )
        scores_txt = jnp.where(valid, scores_txt, -jnp.inf)
        row_max = jnp.maximum(
            jnp.max(scores_img, axis=1, keepdims=True), jnp.max(scores_txt, axis=1, keepdims=True)
        )
        exp_img = jnp.exp(scores_img - row_max)
        exp_txt = jnp.exp(scores_txt - row_max)
        total = jnp.sum(exp_img, axis=1, keepdims=True) + jnp.sum(exp_txt, axis=1, keepdims=True)
        weights_img = (exp_img / total).astype(jnp.bfloat16)
        weights_txt = (exp_txt / total).astype(jnp.bfloat16)
        mixed = jnp.dot(weights_img, values_img, preferred_element_type=jnp.float32) + jnp.dot(
            weights_txt, values_txt, preferred_element_type=jnp.float32
        )
        result = jnp.where(chosen, mixed, result)
    o_ref[...] = result.astype(o_ref.dtype)


def attend_kernel(queries, keys_img, values_img, keys_txt, values_txt, valid):
    return pl.pallas_call(
        attention_kernel,
        out_shape=jax.ShapeDtypeStruct(queries.shape, jnp.bfloat16),
    )(queries, keys_img, values_img, keys_txt, values_txt, valid)


def shifted(value, axis, step):
    size = lax.axis_size(axis)
    return lax.ppermute(value, axis, [(i, (i + step) % size) for i in range(size)])


def shards(
    img_hidden,
    txt_hidden,
    modulation,
    text_lengths,
    timestep_index,
    sigmas,
    latents,
    w_qkv,
    w_kv_text,
    w_out,
    w_up,
    w_down,
    w_final,
):
    img_slice = img_hidden.shape[1]
    requests = img_hidden.shape[2]
    model_width = img_hidden.shape[3]
    txt_slice = txt_hidden.shape[1]
    features = w_out.shape[0]
    members = lax.axis_size("seq") // requests
    parties = lax.axis_size("tp")
    portion = img_slice // parties
    rows_all = img_slice * requests
    adaptive = modulation[0].astype(jnp.float32)
    resident = img_hidden[0].astype(jnp.float32)
    lengths_all = text_lengths[0]
    normed = modulate(resident, adaptive[:, 0], adaptive[:, 1]).reshape(rows_all, model_width)
    queries, keys_img, vals_img = [
        jnp.dot(normed, w_qkv[:, part], preferred_element_type=jnp.float32)
        .astype(jnp.bfloat16)
        .reshape(img_slice, requests, features)
        for part in range(3)
    ]
    text_in = modulate(txt_hidden[0].astype(jnp.float32), adaptive[:, 6], adaptive[:, 7]).reshape(
        txt_slice * requests, model_width
    )
    text_kv = jnp.dot(
        text_in, w_kv_text.reshape(model_width, 2 * features), preferred_element_type=jnp.float32
    ).astype(jnp.bfloat16)
    keys_txt = text_kv[:, :features].reshape(txt_slice, requests, features)
    vals_txt = text_kv[:, features:].reshape(txt_slice, requests, features)
    key_span = img_slice + txt_slice
    senders = requests * members
    halves = members // 2
    query_share = img_slice // halves
    head_share = features // 2
    query_send = (
        queries.reshape(halves, query_share, requests, 2, head_share)
        .transpose(2, 3, 0, 1, 4)
        .reshape(senders, query_share, head_share)
    )
    joined_k = jnp.concatenate([keys_img, keys_txt], 0).reshape(key_span, requests, 2, head_share)
    joined_v = jnp.concatenate([vals_img, vals_txt], 0).reshape(key_span, requests, 2, head_share)
    kv_send = (
        jnp.stack([joined_k, joined_v], 3)
        .transpose(1, 2, 3, 0, 4)
        .reshape(senders, key_span, head_share)
    )
    payload = jnp.concatenate([query_send, kv_send], 1)
    got = lax.all_to_all(payload, "seq", split_axis=0, concat_axis=0, tiled=True)
    query_got = got[:, :query_share]
    kv_mine = got[:, query_share:]
    kv_other = swapped(kv_mine, "seq", 0)
    first_core = lax.axis_index("seq") % 2 == 0
    key_got = jnp.where(first_core, kv_mine, kv_other)
    value_got = jnp.where(first_core, kv_other, kv_mine)
    my_request = lax.axis_index("seq") // members
    length_now = jnp.sum(jnp.where(jnp.arange(requests) == my_request, lengths_all, 0))
    text_rows = senders * txt_slice
    text_span = -(-text_rows // 128) * 128
    text_valid = jnp.arange(text_span) < jnp.minimum(length_now, text_rows)

    def image_part(block):
        return block[:, :img_slice].reshape(senders * img_slice, head_share)

    def text_part(block):
        return jnp.pad(
            block[:, img_slice:].reshape(text_rows, head_share), ((0, text_span - text_rows), (0, 0))
        )

    answer = attend_kernel(
        query_got.reshape(senders * query_share, head_share),
        image_part(key_got),
        image_part(value_got),
        text_part(key_got),
        text_part(value_got),
        text_valid.astype(jnp.float32).reshape(1, text_span),
    )
    answer_back = lax.all_to_all(
        answer.reshape(senders, query_share, head_share),
        "seq",
        split_axis=0,
        concat_axis=0,
        tiled=True,
    )
    attn_rows = (
        answer_back.reshape(requests, 2, halves, query_share, head_share)
        .transpose(2, 3, 0, 1, 4)
        .reshape(rows_all, features)
    )
    tp_index = lax.axis_index("tp")
    resident_mine = lax.dynamic_slice_in_dim(resident, tp_index * portion, portion, 0)
    block_rows = portion * requests
    attn_total = None
    for step in list(range(1, parties)) + [0]:
        rows_for = lax.dynamic_slice_in_dim(
            attn_rows, ((tp_index + step) % parties) * block_rows, block_rows, 0
        )
        part = jnp.dot(rows_for, w_out, preferred_element_type=jnp.float32).astype(jnp.bfloat16)
        if step:
            part = shifted(part, "tp", step)
        attn_total = (
            part.astype(jnp.float32) if attn_total is None else attn_total + part.astype(jnp.float32)
        )
    attn_mixed = attn_total.reshape(portion, requests, model_width)
    after_attn = resident_mine + adaptive[:, 2] * attn_mixed
    mlp_mine = modulate(after_attn, adaptive[:, 3], adaptive[:, 4])
    arrived = [mlp_mine] + [shifted(mlp_mine, "tp", step) for step in range(1, parties)]
    mlp_total = None
    for step, block in enumerate(arrived):
        hidden = jax.nn.gelu(
            jnp.dot(
                block.reshape(portion * requests, model_width),
                w_up,
                preferred_element_type=jnp.float32,
            ),
            approximate=True,
        ).astype(jnp.bfloat16)
        part = jnp.dot(hidden, w_down, preferred_element_type=jnp.float32).astype(jnp.bfloat16)
        if step:
            part = shifted(part, "tp", -step)
        mlp_total = part.astype(jnp.float32) if mlp_total is None else mlp_total + part.astype(jnp.float32)
    mlp_grown = mlp_total.reshape(portion, requests, model_width)
    after_mlp = after_attn + adaptive[:, 5] * mlp_grown
    head_in = modulate(after_mlp, adaptive[:, 8], adaptive[:, 9]).reshape(
        portion * requests, model_width
    )
    velocity_own = jnp.dot(head_in, w_final, preferred_element_type=jnp.float32).reshape(
        portion, requests, w_final.shape[1]
    )
    half_width = w_final.shape[1] // 2
    cfg_index = lax.axis_index("cfg")
    own_kept = lax.dynamic_slice_in_dim(velocity_own, cfg_index * half_width, half_width, 2)
    own_given = lax.dynamic_slice_in_dim(velocity_own, (1 - cfg_index) * half_width, half_width, 2)
    velocity_other = swapped(own_given, "cfg", 0)
    is_first = cfg_index == 0
    guided_cond = jnp.where(is_first, own_kept, velocity_other)
    guided_free = jnp.where(is_first, velocity_other, own_kept)
    velocity = guided_free + GUIDANCE * (guided_cond - guided_free)
    steps_all = jnp.arange(sigmas.shape[0], dtype=jnp.int32)
    sigma_now = jnp.sum(
        jnp.where(steps_all[None, :] == timestep_index[:, None], sigmas[None, :], 0.0), 1
    )
    sigma_after = jnp.sum(
        jnp.where(steps_all[None, :] == timestep_index[:, None] + 1, sigmas[None, :], 0.0), 1
    )
    latent_next = latents + (sigma_after - sigma_now)[None, :, None] * velocity
    return (velocity, latent_next)


def solution(mesh):
    return jax.shard_map(
        shards,
        mesh=mesh,
        in_specs=(
            P("cfg", "seq", None, None),
            P("cfg", "seq", None, None),
            P("cfg", None, None, None),
            P("cfg", None),
            P(),
            P(),
            P(("seq", "tp"), None, "cfg"),
            P(None, None, "tp"),
            P(None, None, "tp"),
            P("tp", None),
            P(None, "tp"),
            P("tp", None),
            P(),
        ),
        out_specs=(P(("seq", "tp"), None, "cfg"), P(("seq", "tp"), None, "cfg")),
        check_vma=False,
    )
```

```python
import math

import jax
import jax.numpy as jnp
from jax import lax
from jax.experimental import pallas as pl
from jax.sharding import PartitionSpec as P

HEAD_DIM = 64


EPSILON = 1e-06
GUIDANCE = 7.0


def swapped(value, axis, apart):
    return lax.ppermute(value, axis, [(i, i ^ 1 << apart) for i in range(lax.axis_size(axis))])


def layer_norm(values):
    center = values - jnp.mean(values, -1, keepdims=True)
    return center * lax.rsqrt(jnp.mean(center * center, -1, keepdims=True) + EPSILON)


def modulate(values, shift_add, scale_mul):
    return (layer_norm(values) * (1.0 + scale_mul) + shift_add).astype(jnp.bfloat16)


def attention_kernel(q_ref, ki_ref, vi_ref, kt_ref, vt_ref, valid_ref, o_ref):
    queries = q_ref[...]
    keys_img = ki_ref[...]
    values_img = vi_ref[...]
    keys_txt = kt_ref[...]
    values_txt = vt_ref[...]
    valid = valid_ref[...] > 0.5
    width = queries.shape[1]
    lane_head = lax.broadcasted_iota(jnp.int32, (1, width), 1) // HEAD_DIM
    contract = (((1,), (1,)), ((), ()))
    scale = 1.0 / math.sqrt(HEAD_DIM)
    result = jnp.zeros(o_ref.shape, jnp.float32)
    for head in range(width // HEAD_DIM):
        chosen = lane_head == head
        query_head = jnp.where(chosen, queries, jnp.zeros_like(queries))
        scores_img = (
            lax.dot_general(query_head, keys_img, contract, preferred_element_type=jnp.float32)
            * scale
        )
        scores_txt = (
            lax.dot_general(query_head, keys_txt, contract, preferred_element_type=jnp.float32)
            * scale
        )
        scores_txt = jnp.where(valid, scores_txt, -jnp.inf)
        row_max = jnp.maximum(
            jnp.max(scores_img, axis=1, keepdims=True), jnp.max(scores_txt, axis=1, keepdims=True)
        )
        exp_img = jnp.exp(scores_img - row_max)
        exp_txt = jnp.exp(scores_txt - row_max)
        total = jnp.sum(exp_img, axis=1, keepdims=True) + jnp.sum(exp_txt, axis=1, keepdims=True)
        weights_img = (exp_img / total).astype(jnp.bfloat16)
        weights_txt = (exp_txt / total).astype(jnp.bfloat16)
        mixed = jnp.dot(weights_img, values_img, preferred_element_type=jnp.float32) + jnp.dot(
            weights_txt, values_txt, preferred_element_type=jnp.float32
        )
        result = jnp.where(chosen, mixed, result)
    o_ref[...] = result.astype(o_ref.dtype)


def attend_kernel(queries, keys_img, values_img, keys_txt, values_txt, valid):
    return pl.pallas_call(
        attention_kernel,
        out_shape=jax.ShapeDtypeStruct(queries.shape, jnp.bfloat16),
    )(queries, keys_img, values_img, keys_txt, values_txt, valid)


def shifted(value, axis, step):
    size = lax.axis_size(axis)
    return lax.ppermute(value, axis, [(i, (i + step) % size) for i in range(size)])


def shards(
    img_hidden,
    txt_hidden,
    modulation,
    text_lengths,
    timestep_index,
    sigmas,
    latents,
    w_qkv,
    w_kv_text,
    w_out,
    w_up,
    w_down,
    w_final,
):
    img_slice = img_hidden.shape[1]
    requests = img_hidden.shape[2]
    model_width = img_hidden.shape[3]
    txt_slice = txt_hidden.shape[1]
    features = w_out.shape[0]
    members = lax.axis_size("seq") // requests
    parties = lax.axis_size("tp")
    portion = img_slice // parties
    rows_all = img_slice * requests
    adaptive = modulation[0].astype(jnp.float32)
    resident = img_hidden[0].astype(jnp.float32)
    lengths_all = text_lengths[0]
    normed = modulate(resident, adaptive[:, 0], adaptive[:, 1]).reshape(rows_all, model_width)
    queries, keys_img, vals_img = [
        jnp.dot(normed, w_qkv[:, part], preferred_element_type=jnp.float32)
        .astype(jnp.bfloat16)
        .reshape(img_slice, requests, features)
        for part in range(3)
    ]
    text_in = modulate(txt_hidden[0].astype(jnp.float32), adaptive[:, 6], adaptive[:, 7]).reshape(
        txt_slice * requests, model_width
    )
    text_kv = jnp.dot(
        text_in, w_kv_text.reshape(model_width, 2 * features), preferred_element_type=jnp.float32
    ).astype(jnp.bfloat16)
    keys_txt = text_kv[:, :features].reshape(txt_slice, requests, features)
    vals_txt = text_kv[:, features:].reshape(txt_slice, requests, features)
    key_span = img_slice + txt_slice
    senders = requests * members
    halves = members // 2
    query_share = img_slice // halves
    head_share = features // 2
    query_send = (
        queries.reshape(halves, query_share, requests, 2, head_share)
        .transpose(2, 3, 0, 1, 4)
        .reshape(senders, query_share, head_share)
    )
    joined_k = jnp.concatenate([keys_img, keys_txt], 0).reshape(key_span, requests, 2, head_share)
    joined_v = jnp.concatenate([vals_img, vals_txt], 0).reshape(key_span, requests, 2, head_share)
    kv_send = (
        jnp.stack([joined_k, joined_v], 3)
        .transpose(1, 2, 3, 0, 4)
        .reshape(senders, key_span, head_share)
    )
    payload = jnp.concatenate([query_send, kv_send], 1)
    got = lax.all_to_all(payload, "seq", split_axis=0, concat_axis=0, tiled=True)
    query_got = got[:, :query_share]
    kv_mine = got[:, query_share:]
    kv_other = swapped(kv_mine, "seq", 0)
    first_core = lax.axis_index("seq") % 2 == 0
    key_got = jnp.where(first_core, kv_mine, kv_other)
    value_got = jnp.where(first_core, kv_other, kv_mine)
    my_request = lax.axis_index("seq") // members
    length_now = jnp.sum(jnp.where(jnp.arange(requests) == my_request, lengths_all, 0))
    text_rows = senders * txt_slice
    text_span = -(-text_rows // 128) * 128
    text_valid = jnp.arange(text_span) < jnp.minimum(length_now, text_rows)

    def image_part(block):
        return block[:, :img_slice].reshape(senders * img_slice, head_share)

    def text_part(block):
        return jnp.pad(
            block[:, img_slice:].reshape(text_rows, head_share), ((0, text_span - text_rows), (0, 0))
        )

    answer = attend_kernel(
        query_got.reshape(senders * query_share, head_share),
        image_part(key_got),
        image_part(value_got),
        text_part(key_got),
        text_part(value_got),
        text_valid.astype(jnp.float32).reshape(1, text_span),
    )
    answer_back = lax.all_to_all(
        answer.reshape(senders, query_share, head_share),
        "seq",
        split_axis=0,
        concat_axis=0,
        tiled=True,
    )
    attn_rows = (
        answer_back.reshape(requests, 2, halves, query_share, head_share)
        .transpose(2, 3, 0, 1, 4)
        .reshape(rows_all, features)
    )
    tp_index = lax.axis_index("tp")
    resident_mine = lax.dynamic_slice_in_dim(resident, tp_index * portion, portion, 0)
    block_rows = portion * requests
    attn_total = None
    for step in range(parties):
        rows_for = lax.dynamic_slice_in_dim(
            attn_rows, ((tp_index + step) % parties) * block_rows, block_rows, 0
        )
        part = jnp.dot(rows_for, w_out, preferred_element_type=jnp.float32).astype(jnp.bfloat16)
        if step:
            part = shifted(part, "tp", step)
        attn_total = (
            part.astype(jnp.float32) if attn_total is None else attn_total + part.astype(jnp.float32)
        )
    attn_mixed = attn_total.reshape(portion, requests, model_width)
    after_attn = resident_mine + adaptive[:, 2] * attn_mixed
    mlp_mine = modulate(after_attn, adaptive[:, 3], adaptive[:, 4])
    arrived = [mlp_mine] + [shifted(mlp_mine, "tp", step) for step in range(1, parties)]
    mlp_total = None
    for step, block in enumerate(arrived):
        hidden = jax.nn.gelu(
            jnp.dot(
                block.reshape(portion * requests, model_width),
                w_up,
                preferred_element_type=jnp.float32,
            ),
            approximate=True,
        ).astype(jnp.bfloat16)
        part = jnp.dot(hidden, w_down, preferred_element_type=jnp.float32).astype(jnp.bfloat16)
        if step:
            part = shifted(part, "tp", -step)
        mlp_total = part.astype(jnp.float32) if mlp_total is None else mlp_total + part.astype(jnp.float32)
    mlp_grown = mlp_total.reshape(portion, requests, model_width)
    after_mlp = after_attn + adaptive[:, 5] * mlp_grown
    head_in = modulate(after_mlp, adaptive[:, 8], adaptive[:, 9]).reshape(
        portion * requests, model_width
    )
    half_width = w_final.shape[1] // 2
    cfg_index = lax.axis_index("cfg")

    def head_columns(start):
        columns = lax.dynamic_slice_in_dim(w_final, start * half_width, half_width, 1)
        return jnp.dot(head_in, columns, preferred_element_type=jnp.float32).reshape(
            portion, requests, half_width
        )

    own_given = head_columns(1 - cfg_index)
    velocity_other = swapped(own_given, "cfg", 0)
    own_kept = head_columns(cfg_index)
    is_first = cfg_index == 0
    guided_cond = jnp.where(is_first, own_kept, velocity_other)
    guided_free = jnp.where(is_first, velocity_other, own_kept)
    velocity = guided_free + GUIDANCE * (guided_cond - guided_free)
    steps_all = jnp.arange(sigmas.shape[0], dtype=jnp.int32)
    sigma_now = jnp.sum(
        jnp.where(steps_all[None, :] == timestep_index[:, None], sigmas[None, :], 0.0), 1
    )
    sigma_after = jnp.sum(
        jnp.where(steps_all[None, :] == timestep_index[:, None] + 1, sigmas[None, :], 0.0), 1
    )
    latent_next = latents + (sigma_after - sigma_now)[None, :, None] * velocity
    return (velocity, latent_next)


def solution(mesh):
    return jax.shard_map(
        shards,
        mesh=mesh,
        in_specs=(
            P("cfg", "seq", None, None),
            P("cfg", "seq", None, None),
            P("cfg", None, None, None),
            P("cfg", None),
            P(),
            P(),
            P(("seq", "tp"), None, "cfg"),
            P(None, None, "tp"),
            P(None, None, "tp"),
            P("tp", None),
            P(None, "tp"),
            P("tp", None),
            P(),
        ),
        out_specs=(P(("seq", "tp"), None, "cfg"), P(("seq", "tp"), None, "cfg")),
        check_vma=False,
    )
```

```python
import math

import jax
import jax.numpy as jnp
from jax import lax
from jax.experimental import pallas as pl
from jax.sharding import PartitionSpec as P

HEAD_DIM = 64


EPSILON = 1e-06
GUIDANCE = 7.0


def swapped(value, axis, apart):
    return lax.ppermute(value, axis, [(i, i ^ 1 << apart) for i in range(lax.axis_size(axis))])


def layer_norm(values):
    center = values - jnp.mean(values, -1, keepdims=True)
    return center * lax.rsqrt(jnp.mean(center * center, -1, keepdims=True) + EPSILON)


def modulate(values, shift_add, scale_mul):
    return (layer_norm(values) * (1.0 + scale_mul) + shift_add).astype(jnp.bfloat16)


def attention_kernel(q_ref, ki_ref, vi_ref, kt_ref, vt_ref, valid_ref, o_ref):
    queries = q_ref[...]
    keys_img = ki_ref[...]
    values_img = vi_ref[...]
    keys_txt = kt_ref[...]
    values_txt = vt_ref[...]
    valid = valid_ref[...] > 0.5
    width = queries.shape[1]
    lane_head = lax.broadcasted_iota(jnp.int32, (1, width), 1) // HEAD_DIM
    contract = (((1,), (1,)), ((), ()))
    scale = 1.0 / math.sqrt(HEAD_DIM)
    result = jnp.zeros(o_ref.shape, jnp.float32)
    for head in range(width // HEAD_DIM):
        chosen = lane_head == head
        query_head = jnp.where(chosen, queries, jnp.zeros_like(queries))
        scores_img = (
            lax.dot_general(query_head, keys_img, contract, preferred_element_type=jnp.float32)
            * scale
        )
        scores_txt = (
            lax.dot_general(query_head, keys_txt, contract, preferred_element_type=jnp.float32)
            * scale
        )
        scores_txt = jnp.where(valid, scores_txt, -jnp.inf)
        row_max = jnp.maximum(
            jnp.max(scores_img, axis=1, keepdims=True), jnp.max(scores_txt, axis=1, keepdims=True)
        )
        exp_img = jnp.exp(scores_img - row_max)
        exp_txt = jnp.exp(scores_txt - row_max)
        total = jnp.sum(exp_img, axis=1, keepdims=True) + jnp.sum(exp_txt, axis=1, keepdims=True)
        weights_img = (exp_img / total).astype(jnp.bfloat16)
        weights_txt = (exp_txt / total).astype(jnp.bfloat16)
        mixed = jnp.dot(weights_img, values_img, preferred_element_type=jnp.float32) + jnp.dot(
            weights_txt, values_txt, preferred_element_type=jnp.float32
        )
        result = jnp.where(chosen, mixed, result)
    o_ref[...] = result.astype(o_ref.dtype)


def attend_kernel(queries, keys_img, values_img, keys_txt, values_txt, valid):
    return pl.pallas_call(
        attention_kernel,
        out_shape=jax.ShapeDtypeStruct(queries.shape, jnp.bfloat16),
    )(queries, keys_img, values_img, keys_txt, values_txt, valid)


def shifted(value, axis, step):
    size = lax.axis_size(axis)
    return lax.ppermute(value, axis, [(i, (i + step) % size) for i in range(size)])


def shards(
    img_hidden,
    txt_hidden,
    modulation,
    text_lengths,
    timestep_index,
    sigmas,
    latents,
    w_qkv,
    w_kv_text,
    w_out,
    w_up,
    w_down,
    w_final,
):
    img_slice = img_hidden.shape[1]
    requests = img_hidden.shape[2]
    model_width = img_hidden.shape[3]
    txt_slice = txt_hidden.shape[1]
    features = w_out.shape[0]
    members = lax.axis_size("seq") // requests
    parties = lax.axis_size("tp")
    portion = img_slice // parties
    rows_all = img_slice * requests
    adaptive = modulation[0].astype(jnp.float32)
    resident = img_hidden[0].astype(jnp.float32)
    lengths_all = text_lengths[0]
    normed = modulate(resident, adaptive[:, 0], adaptive[:, 1]).reshape(rows_all, model_width)
    queries, keys_img, vals_img = [
        jnp.dot(normed, w_qkv[:, part], preferred_element_type=jnp.float32)
        .astype(jnp.bfloat16)
        .reshape(img_slice, requests, features)
        for part in range(3)
    ]
    text_in = modulate(txt_hidden[0].astype(jnp.float32), adaptive[:, 6], adaptive[:, 7]).reshape(
        txt_slice * requests, model_width
    )
    text_kv = jnp.dot(
        text_in, w_kv_text.reshape(model_width, 2 * features), preferred_element_type=jnp.float32
    ).astype(jnp.bfloat16)
    keys_txt = text_kv[:, :features].reshape(txt_slice, requests, features)
    vals_txt = text_kv[:, features:].reshape(txt_slice, requests, features)
    key_span = img_slice + txt_slice
    senders = requests * members
    halves = members // 2
    query_share = img_slice // halves
    head_share = features // 2
    query_send = (
        queries.reshape(halves, query_share, requests, 2, head_share)
        .transpose(2, 3, 0, 1, 4)
        .reshape(senders, query_share, head_share)
    )
    joined_k = jnp.concatenate([keys_img, keys_txt], 0).reshape(key_span, requests, 2, head_share)
    joined_v = jnp.concatenate([vals_img, vals_txt], 0).reshape(key_span, requests, 2, head_share)
    kv_send = (
        jnp.stack([joined_k, joined_v], 3)
        .transpose(1, 2, 3, 0, 4)
        .reshape(senders, key_span, head_share)
    )
    payload = jnp.concatenate([query_send, kv_send], 1)
    got = lax.all_to_all(payload, "seq", split_axis=0, concat_axis=0, tiled=True)
    query_got = got[:, :query_share]
    kv_mine = got[:, query_share:]
    kv_other = swapped(kv_mine, "seq", 0)
    first_core = lax.axis_index("seq") % 2 == 0
    key_got = jnp.where(first_core, kv_mine, kv_other)
    value_got = jnp.where(first_core, kv_other, kv_mine)
    my_request = lax.axis_index("seq") // members
    length_now = jnp.sum(jnp.where(jnp.arange(requests) == my_request, lengths_all, 0))
    text_rows = senders * txt_slice
    text_span = -(-text_rows // 128) * 128
    text_valid = jnp.arange(text_span) < jnp.minimum(length_now, text_rows)

    def image_part(block):
        return block[:, :img_slice].reshape(senders * img_slice, head_share)

    def text_part(block):
        return jnp.pad(
            block[:, img_slice:].reshape(text_rows, head_share), ((0, text_span - text_rows), (0, 0))
        )

    answer = attend_kernel(
        query_got.reshape(senders * query_share, head_share),
        image_part(key_got),
        image_part(value_got),
        text_part(key_got),
        text_part(value_got),
        text_valid.astype(jnp.float32).reshape(1, text_span),
    )
    answer_back = lax.all_to_all(
        answer.reshape(senders, query_share, head_share),
        "seq",
        split_axis=0,
        concat_axis=0,
        tiled=True,
    )
    attn_rows = (
        answer_back.reshape(requests, 2, halves, query_share, head_share)
        .transpose(2, 3, 0, 1, 4)
        .reshape(rows_all, features)
    )
    tp_index = lax.axis_index("tp")
    resident_mine = lax.dynamic_slice_in_dim(resident, tp_index * portion, portion, 0)
    block_rows = portion * requests
    attn_total = None
    attn_whole = jnp.dot(attn_rows, w_out, preferred_element_type=jnp.float32).astype(jnp.bfloat16)
    for step in range(parties):
        part = lax.dynamic_slice_in_dim(
            attn_whole, ((tp_index + step) % parties) * block_rows, block_rows, 0
        )
        if step:
            part = shifted(part, "tp", step)
        attn_total = (
            part.astype(jnp.float32) if attn_total is None else attn_total + part.astype(jnp.float32)
        )
    attn_mixed = attn_total.reshape(portion, requests, model_width)
    after_attn = resident_mine + adaptive[:, 2] * attn_mixed
    mlp_mine = modulate(after_attn, adaptive[:, 3], adaptive[:, 4])
    arrived = [mlp_mine] + [shifted(mlp_mine, "tp", step) for step in range(1, parties)]
    mlp_total = None
    for step, block in enumerate(arrived):
        hidden = jax.nn.gelu(
            jnp.dot(
                block.reshape(portion * requests, model_width),
                w_up,
                preferred_element_type=jnp.float32,
            ),
            approximate=True,
        ).astype(jnp.bfloat16)
        part = jnp.dot(hidden, w_down, preferred_element_type=jnp.float32).astype(jnp.bfloat16)
        if step:
            part = shifted(part, "tp", -step)
        mlp_total = part.astype(jnp.float32) if mlp_total is None else mlp_total + part.astype(jnp.float32)
    mlp_grown = mlp_total.reshape(portion, requests, model_width)
    after_mlp = after_attn + adaptive[:, 5] * mlp_grown
    head_in = modulate(after_mlp, adaptive[:, 8], adaptive[:, 9]).reshape(
        portion * requests, model_width
    )
    velocity_own = jnp.dot(head_in, w_final, preferred_element_type=jnp.float32).reshape(
        portion, requests, w_final.shape[1]
    )
    half_width = w_final.shape[1] // 2
    cfg_index = lax.axis_index("cfg")
    own_kept = lax.dynamic_slice_in_dim(velocity_own, cfg_index * half_width, half_width, 2)
    own_given = lax.dynamic_slice_in_dim(velocity_own, (1 - cfg_index) * half_width, half_width, 2)
    velocity_other = swapped(own_given, "cfg", 0)
    is_first = cfg_index == 0
    guided_cond = jnp.where(is_first, own_kept, velocity_other)
    guided_free = jnp.where(is_first, velocity_other, own_kept)
    velocity = guided_free + GUIDANCE * (guided_cond - guided_free)
    steps_all = jnp.arange(sigmas.shape[0], dtype=jnp.int32)
    sigma_now = jnp.sum(
        jnp.where(steps_all[None, :] == timestep_index[:, None], sigmas[None, :], 0.0), 1
    )
    sigma_after = jnp.sum(
        jnp.where(steps_all[None, :] == timestep_index[:, None] + 1, sigmas[None, :], 0.0), 1
    )
    latent_next = latents + (sigma_after - sigma_now)[None, :, None] * velocity
    return (velocity, latent_next)


def solution(mesh):
    return jax.shard_map(
        shards,
        mesh=mesh,
        in_specs=(
            P("cfg", "seq", None, None),
            P("cfg", "seq", None, None),
            P("cfg", None, None, None),
            P("cfg", None),
            P(),
            P(),
            P(("seq", "tp"), None, "cfg"),
            P(None, None, "tp"),
            P(None, None, "tp"),
            P("tp", None),
            P(None, "tp"),
            P("tp", None),
            P(),
        ),
        out_specs=(P(("seq", "tp"), None, "cfg"), P(("seq", "tp"), None, "cfg")),
        check_vma=False,
    )
```
